32 devices in a mesh: sec: 2 (over x), seq: 8 (over z, core), mp: 2 (over y).
Axes of the slice: x: 2, y: 2, z: 4, core: 2. Of those that a mesh axis runs over, the one named last changes fastest.
Arguments:
- heads_in: bfloat16 [2, 2, 3072, 2048], P('sec', None, 'seq', 'mp'), may hold values from -8 to 8
- doc_units: int32 [12], replicated, may hold values from 1 to 3, 24 in all
Outputs:
- results: bfloat16 [2, 2, 3072, 2048], P('sec', None, 'seq', 'mp')
The draws below stay inside these ranges and needn't reach their ends.
Inputs may be any that keep to these rules, and one draw needn't show every extreme that they name: `doc_units`: lengths of 12 packed documents in steps of 128 tokens, summing to 24; the longest is exactly 3 steps.
All inputs are finite; a program needn't handle non-finite values.
Results may differ from the reference program's by a relative error of at most 0.0084.
Values may be sent and summed in bfloat16 or wider, within the bound.
No kernel may reach another device: no remote copies, remote signals or barrier semaphores. Data moves between devices by JAX's collectives and lax.ppermute only.
A program may use at most 128 MiB of HBM per device.

```python
import math
import jax
import jax.numpy as jnp
import numpy as np
from jax import lax

TOK_DEV = 384
UNIT = 128
HEADS = 32
DH = 64
TOKENS = 3072
UNITS = 24
NDOCS = 12
N_SEQ = 8


def draw_heads_in(key, part):
    columns = HEADS * DH
    key_base = jax.random.fold_in(jax.random.fold_in(key, 11), 0)
    key_values = jax.random.fold_in(key_base, 3)
    head_level = (jnp.arange(columns) // DH).astype(jnp.float32) / max(HEADS - 1, 1)
    shape = (3, TOKENS, columns)
    base = jnp.clip(jax.random.normal(key_base, shape, jnp.float32), -4.0, 4.0)
    values = jnp.clip(jax.random.normal(key_values, (TOKENS, columns), jnp.float32), -2.0, 2.0) * (0.4 * 10.0 ** head_level)[None, :]
    keys = base[0]
    queries = base[1]
    cotangent = base[2]
    return jnp.stack([jnp.stack([keys, values]), jnp.stack([queries, cotangent])]).astype(jnp.bfloat16)


def length_profile(number_of, total, bound, skew):
    portions = [(1 << 20) // math.isqrt(grade ** skew) + 1 for grade in range(2, number_of + 1)]
    rest, given = total - bound - (number_of - 1), [1] * (number_of - 1)
    while rest > 0:
        movable = [i for i in range(number_of - 1) if given[i] < bound]
        whole, budget = sum([portions[i] for i in movable]), rest
        for i in movable:
            extra = min(bound - given[i], max(1, budget * portions[i] // whole), rest)
            given[i] = given[i] + extra
            rest = rest - extra
    return np.array([bound] + given)


def ragged_sizes(own_key, count, total, reach, lean):
    if count == 2:
        one = jax.random.randint(own_key, (), max(1, total - reach), min(reach, total - 1) + 1)
        return jnp.stack([one, total - one])
    lengths = jnp.asarray(length_profile(count, total, reach, lean), jnp.int32)
    twos = (count - 1) // 2
    source_of, sink = lengths[1:1 + 2 * twos:2], lengths[2:2 + 2 * twos:2]
    margin = jnp.minimum(source_of - 1, reach - sink)
    passed = jax.random.randint(jax.random.fold_in(own_key, 1), (twos,), 0, 1 << 20) % (margin + 1)
    lengths = lengths.at[1:1 + 2 * twos:2].set(source_of - passed).at[2:2 + 2 * twos:2].set(sink + passed)
    return lengths[jax.random.permutation(jax.random.fold_in(own_key, 2), count)]


def setup_inputs(seed: int = 0) -> dict:
    seeds = jax.random.split(jax.random.key(seed), 3)
    return {
        "heads_in": draw_heads_in(jax.random.fold_in(seeds[2], 71), 0),
        "doc_units": ragged_sizes(seeds[1], NDOCS, UNITS, TOK_DEV // UNIT, 1).astype(jnp.int32),
    }


epsilon = 1e-06

def doc_index(positions, doc_ends):
    counted = lax.optimization_barrier(jnp.sum((doc_ends[None, :] <= positions[:, None]).astype(jnp.int32), axis=1)).astype(jnp.int32)
    return jnp.where(positions < 0, jnp.int32(-1), counted).astype(jnp.int32)

def probabilities(query_head, key_head, allowed, score_scale):
    scores = lax.dot_general(query_head, key_head, (((1,), (1,)), ((), ())), preferred_element_type=jnp.float32) * score_scale
    scores = jnp.where(allowed, scores, -jnp.inf)
    row_max = lax.optimization_barrier(jnp.max(scores, axis=1, keepdims=True))
    expven = jnp.exp(scores - row_max)
    return expven / lax.optimization_barrier(jnp.sum(expven, axis=1, keepdims=True))

def block_grads(queries, cotangent, keys, values, allowed, total_fn):
    head_cols = queries.shape[1]
    score_scale = DH ** (-0.5)
    pieces = []
    for head_index in range(head_cols // DH):
        cols = slice(head_index * DH, (head_index + 1) * DH)
        weights = probabilities(queries[:, cols], keys[:, cols], allowed, score_scale)
        pieces.append(jnp.dot(weights.astype(jnp.bfloat16), values[:, cols], preferred_element_type=jnp.float32))
    attended = jnp.concatenate(pieces, axis=1)
    cot_float = cotangent.astype(jnp.float32)
    squares, crosses = total_fn((lax.optimization_barrier(jnp.sum(attended * attended, axis=1)), lax.optimization_barrier(jnp.sum(cot_float * attended, axis=1))))
    spread = jnp.sqrt(squares / (HEADS * DH) + epsilon)
    normed = attended / spread[:, None]
    shared = crosses / (HEADS * DH) / spread
    upstream = lax.optimization_barrier(((cot_float - normed * shared[:, None]) / spread[:, None]).astype(jnp.bfloat16))
    grad_query, grad_key, grad_value = ([], [], [])
    for head_index in range(head_cols // DH):
        cols = slice(head_index * DH, (head_index + 1) * DH)
        weights = probabilities(queries[:, cols], keys[:, cols], allowed, score_scale)
        rounded = weights.astype(jnp.bfloat16)
        up_head = upstream[:, cols]
        delta = lax.optimization_barrier(jnp.sum(up_head.astype(jnp.float32) * attended[:, cols], axis=1))
        dprobs = lax.dot_general(up_head, values[:, cols], (((1,), (1,)), ((), ())), preferred_element_type=jnp.float32)
        dscores = (weights * (dprobs - delta[:, None]) * score_scale).astype(jnp.bfloat16)
        grad_query.append(jnp.dot(dscores, keys[:, cols], preferred_element_type=jnp.float32))
        grad_key.append(lax.dot_general(dscores, queries[:, cols], (((0,), (0,)), ((), ())), preferred_element_type=jnp.float32))
        grad_value.append(lax.dot_general(rounded, up_head, (((0,), (0,)), ((), ())), preferred_element_type=jnp.float32))
    return (jnp.concatenate(grad_query, axis=1), normed, jnp.concatenate(grad_key, axis=1), jnp.concatenate(grad_value, axis=1))

def keep_sums(sums_pair):
    return sums_pair

def reference(heads_in, doc_units):
    keys_all = heads_in[0, 0]
    values_all = heads_in[0, 1]
    queries_all = heads_in[1, 0]
    cot_all = heads_in[1, 1]
    row_count = TOK_DEV
    head_cols = HEADS * DH
    doc_ends = (jnp.cumsum(doc_units).astype(jnp.int32) * UNIT).astype(jnp.int32)
    padding = jnp.zeros((row_count, head_cols), heads_in.dtype)
    keys_pad = jnp.concatenate([padding, keys_all, padding], axis=0)
    values_pad = jnp.concatenate([padding, values_all, padding], axis=0)

    def block_step(totals, block_number):
        key_total, value_total = totals
        start = (block_number * row_count).astype(jnp.int32)
        queries = lax.dynamic_slice_in_dim(queries_all, start, row_count, 0)
        cotangent = lax.dynamic_slice_in_dim(cot_all, start, row_count, 0)
        keys = lax.dynamic_slice_in_dim(keys_pad, start, 3 * row_count, 0)
        values = lax.dynamic_slice_in_dim(values_pad, start, 3 * row_count, 0)
        query_pos = start + jnp.arange(row_count, dtype=jnp.int32)
        key_pos = start - row_count + jnp.arange(3 * row_count, dtype=jnp.int32)
        allowed = doc_index(query_pos, doc_ends)[:, None] == doc_index(key_pos, doc_ends)[None, :]
        grad_q, normed, grad_k, grad_v = block_grads(queries, cotangent, keys, values, allowed, keep_sums)
        key_total = lax.dynamic_update_slice_in_dim(key_total, lax.dynamic_slice_in_dim(key_total, start, 3 * row_count, 0) + grad_k, start, 0)
        value_total = lax.dynamic_update_slice_in_dim(value_total, lax.dynamic_slice_in_dim(value_total, start, 3 * row_count, 0) + grad_v, start, 0)
        return ((key_total, value_total), (grad_q.astype(jnp.bfloat16), normed.astype(jnp.bfloat16)))
    zeros_pad = jnp.zeros((TOKENS + 2 * row_count, head_cols), jnp.float32)
    (key_total, value_total), (query_blocks, normed_blocks) = lax.scan(block_step, (zeros_pad, zeros_pad), jnp.arange(N_SEQ, dtype=jnp.int32))
    grad_k = key_total[row_count:row_count + TOKENS].astype(jnp.bfloat16)
    grad_v = value_total[row_count:row_count + TOKENS].astype(jnp.bfloat16)
    grad_q = query_blocks.reshape(TOKENS, head_cols)
    normed = normed_blocks.reshape(TOKENS, head_cols)
    return jnp.stack([jnp.stack([grad_k, grad_v]), jnp.stack([grad_q, normed])])
```

```python
import jax
import jax.numpy as jnp
from jax import lax
from jax.sharding import PartitionSpec as P

UNIT = 128
HEADS = 32
DH = 64
MAX_DOC_UNITS = 3


epsilon = 1e-06


def seq_shift(value, steps):
    count = lax.axis_size("seq")
    initial, last = (max(0, -steps), min(count, count - steps))
    return lax.ppermute(value, "seq", [(source, source + steps) for source in range(initial, last)])


def sec_swap(value):
    return lax.ppermute(value, "sec", [(0, 1), (1, 0)])


def window_plan(doc_units, seq_place, unit_count, halo_units):
    ends = jnp.cumsum(doc_units).astype(jnp.int32)
    first_unit = seq_place * unit_count
    query_units = first_unit + jnp.arange(unit_count, dtype=jnp.int32)

    def unit_doc(units):
        counted = jnp.sum((ends[None, :] <= units[:, None]).astype(jnp.int32), axis=1)
        return jnp.where(units < 0, jnp.int32(-1), counted)

    starts = jnp.max(
        jnp.where(ends[None, :] <= query_units[:, None], ends[None, :], 0), axis=1
    ).astype(jnp.int32)
    key_units = starts[:, None] + jnp.arange(MAX_DOC_UNITS, dtype=jnp.int32)[None, :]
    allowed = unit_doc(key_units.reshape(-1)).reshape(key_units.shape) == unit_doc(query_units)[:, None]
    return starts - (first_unit - halo_units), allowed


def attention_grads(queries, cotangent, near_keys, near_values, rel_starts, allowed, total_fn, total_cols):
    rows, head_cols = queries.shape
    heads = head_cols // DH
    unit_count = rows // UNIT
    window = MAX_DOC_UNITS * UNIT
    score_scale = DH ** (-0.5)

    def windows(near):
        pieces = [
            lax.dynamic_slice_in_dim(near, rel_starts[j] * UNIT, window, 0) for j in range(unit_count)
        ]
        return jnp.stack(pieces).reshape(unit_count, window, heads, DH)

    keys_w = windows(near_keys)
    values_w = windows(near_values)
    q4 = queries.reshape(unit_count, UNIT, heads, DH)
    cot_float = cotangent.astype(jnp.float32)

    mask = jnp.repeat(allowed, UNIT, axis=1)[:, None, None, :]
    scores = (
        jnp.einsum("jqhd,jkhd->jhqk", q4, keys_w, preferred_element_type=jnp.float32) * score_scale
    )
    scores = jnp.where(mask, scores, -jnp.inf)
    row_max = jnp.max(scores, axis=3, keepdims=True)
    expven = jnp.exp(scores - row_max)
    weights = expven / jnp.sum(expven, axis=3, keepdims=True)
    rounded = weights.astype(jnp.bfloat16)
    attended4 = jnp.einsum("jhqk,jkhd->jqhd", rounded, values_w, preferred_element_type=jnp.float32)
    attended = attended4.reshape(rows, head_cols)

    squares, crosses = total_fn(
        (jnp.sum(attended * attended, axis=1), jnp.sum(cot_float * attended, axis=1))
    )
    spread = jnp.sqrt(squares / total_cols + epsilon)
    normed = attended / spread[:, None]
    shared = crosses / total_cols / spread
    upstream = ((cot_float - normed * shared[:, None]) / spread[:, None]).astype(jnp.bfloat16)
    up4 = upstream.reshape(unit_count, UNIT, heads, DH)

    delta = jnp.sum(up4.astype(jnp.float32) * attended4, axis=3)
    delta = jnp.transpose(delta, (0, 2, 1))[..., None]
    dprobs = jnp.einsum("jqhd,jkhd->jhqk", up4, values_w, preferred_element_type=jnp.float32)
    dscores = (weights * (dprobs - delta) * score_scale).astype(jnp.bfloat16)
    grad_q = jnp.einsum("jhqk,jkhd->jqhd", dscores, keys_w, preferred_element_type=jnp.float32)
    grad_kw = jnp.einsum("jhqk,jqhd->jkhd", dscores, q4, preferred_element_type=jnp.float32)
    grad_vw = jnp.einsum("jhqk,jqhd->jkhd", rounded, up4, preferred_element_type=jnp.float32)
    grad_kvw = jnp.concatenate(
        [grad_kw.reshape(unit_count, window, head_cols), grad_vw.reshape(unit_count, window, head_cols)],
        axis=2,
    )
    near_rows = near_keys.shape[0]
    total = jnp.zeros((near_rows, 2 * head_cols), jnp.float32)
    for j in range(unit_count):
        start = rel_starts[j] * UNIT
        total = lax.dynamic_update_slice_in_dim(
            total, lax.dynamic_slice_in_dim(total, start, window, 0) + grad_kvw[j], start, 0
        )
    return grad_q.reshape(rows, head_cols), normed, total


def per_device(heads_in, doc_units):
    section = lax.axis_index("sec")
    seq_place = lax.axis_index("seq")
    is_first = section == 0
    local_heads = heads_in[0]
    _, rows, cols = local_heads.shape
    half = cols // 2
    unit_count = rows // UNIT
    halo_units = MAX_DOC_UNITS - 1
    halo = halo_units * UNIT
    total_cols = cols * lax.axis_size("mp")

    keep_offset = section * half
    send_offset = (1 - section) * half
    sent = lax.dynamic_slice_in_dim(local_heads, send_offset, half, 2)
    kept = lax.dynamic_slice_in_dim(local_heads, keep_offset, half, 2)
    arrived = sec_swap(sent)
    key_value = jnp.where(is_first, kept, arrived)
    query_cot = jnp.where(is_first, arrived, kept)

    joined = jnp.concatenate([key_value[0], key_value[1]], axis=1)
    low = seq_shift(joined[rows - halo :], 1)
    high = seq_shift(joined[:halo], -1)
    near = jnp.concatenate([low, joined, high], axis=0)

    rel_starts, allowed = window_plan(doc_units, seq_place, unit_count, halo_units)

    def row_total(sums_pair):
        return lax.psum(sums_pair, ("sec", "mp"))

    grad_q, normed, total = attention_grads(
        query_cot[0],
        query_cot[1],
        near[:, :half],
        near[:, half:],
        rel_starts,
        allowed,
        row_total,
        total_cols,
    )
    from_left = seq_shift(total[near.shape[0] - halo :], 1)
    from_right = seq_shift(total[:halo], -1)
    own = total[halo : halo + rows]
    own = own.at[:halo].add(from_left)
    own = own.at[rows - halo :].add(from_right)
    grad_k = own[:, :half].astype(jnp.bfloat16)
    grad_v = own[:, half:].astype(jnp.bfloat16)

    kv_pair = jnp.stack([grad_k, grad_v])
    qn_pair = jnp.stack([grad_q.astype(jnp.bfloat16), normed.astype(jnp.bfloat16)])
    keep_pair = jnp.where(is_first, kv_pair, qn_pair)
    back = sec_swap(jnp.where(is_first, qn_pair, kv_pair))
    result = jnp.where(
        is_first,
        jnp.concatenate([keep_pair, back], axis=2),
        jnp.concatenate([back, keep_pair], axis=2),
    )
    return result[None]


def solution(mesh):
    return jax.shard_map(
        per_device,
        mesh=mesh,
        in_specs=(P("sec", None, "seq", "mp"), P()),
        out_specs=P("sec", None, "seq", "mp"),
        check_vma=False,
    )
```

```python
import jax
import jax.numpy as jnp
from jax import lax
from jax.sharding import PartitionSpec as P

UNIT = 128
HEADS = 32
DH = 64
MAX_DOC_UNITS = 3


epsilon = 1e-06


def seq_shift(value, steps):
    count = lax.axis_size("seq")
    initial, last = (max(0, -steps), min(count, count - steps))
    return lax.ppermute(value, "seq", [(source, source + steps) for source in range(initial, last)])


def sec_swap(value):
    return lax.ppermute(value, "sec", [(0, 1), (1, 0)])


def window_plan(doc_units, seq_place, unit_count, halo_units):
    ends = jnp.cumsum(doc_units).astype(jnp.int32)
    first_unit = seq_place * unit_count
    query_units = first_unit + jnp.arange(unit_count, dtype=jnp.int32)

    def unit_doc(units):
        counted = jnp.sum((ends[None, :] <= units[:, None]).astype(jnp.int32), axis=1)
        return jnp.where(units < 0, jnp.int32(-1), counted)

    starts = jnp.max(
        jnp.where(ends[None, :] <= query_units[:, None], ends[None, :], 0), axis=1
    ).astype(jnp.int32)
    key_units = starts[:, None] + jnp.arange(MAX_DOC_UNITS, dtype=jnp.int32)[None, :]
    allowed = unit_doc(key_units.reshape(-1)).reshape(key_units.shape) == unit_doc(query_units)[:, None]
    return starts - (first_unit - halo_units), allowed


def chunk_forward(queries, cotangent, near_keys, near_values, rel_starts, allowed):
    rows, head_cols = queries.shape
    heads = head_cols // DH
    unit_count = rows // UNIT
    window = MAX_DOC_UNITS * UNIT
    score_scale = DH ** (-0.5)

    def windows(near):
        pieces = [
            lax.dynamic_slice_in_dim(near, rel_starts[j] * UNIT, window, 0) for j in range(unit_count)
        ]
        return jnp.stack(pieces).reshape(unit_count, window, heads, DH)

    keys_w = windows(near_keys)
    values_w = windows(near_values)
    q4 = queries.reshape(unit_count, UNIT, heads, DH)
    cot_float = cotangent.astype(jnp.float32)
    mask = jnp.repeat(allowed, UNIT, axis=1)[:, None, None, :]
    scores = (
        jnp.einsum("jqhd,jkhd->jhqk", q4, keys_w, preferred_element_type=jnp.float32) * score_scale
    )
    scores = jnp.where(mask, scores, -jnp.inf)
    row_max = jnp.max(scores, axis=3, keepdims=True)
    expven = jnp.exp(scores - row_max)
    weights = expven / jnp.sum(expven, axis=3, keepdims=True)
    rounded = weights.astype(jnp.bfloat16)
    attended4 = jnp.einsum("jhqk,jkhd->jqhd", rounded, values_w, preferred_element_type=jnp.float32)
    attended = attended4.reshape(rows, head_cols)
    sums = jnp.stack([jnp.sum(attended * attended, axis=1), jnp.sum(cot_float * attended, axis=1)])
    return (q4, keys_w, values_w, cot_float, weights, rounded, attended4, attended), sums


def chunk_backward(saved, spread, shared, rel_starts, near_rows):
    q4, keys_w, values_w, cot_float, weights, rounded, attended4, attended = saved
    unit_count, _, heads, _ = q4.shape
    rows = unit_count * UNIT
    head_cols = heads * DH
    window = MAX_DOC_UNITS * UNIT
    score_scale = DH ** (-0.5)
    normed = attended / spread[:, None]
    upstream = ((cot_float - normed * shared[:, None]) / spread[:, None]).astype(jnp.bfloat16)
    up4 = upstream.reshape(unit_count, UNIT, heads, DH)
    delta = jnp.sum(up4.astype(jnp.float32) * attended4, axis=3)
    delta = jnp.transpose(delta, (0, 2, 1))[..., None]
    dprobs = jnp.einsum("jqhd,jkhd->jhqk", up4, values_w, preferred_element_type=jnp.float32)
    dscores = (weights * (dprobs - delta) * score_scale).astype(jnp.bfloat16)
    grad_q = jnp.einsum("jhqk,jkhd->jqhd", dscores, keys_w, preferred_element_type=jnp.float32)
    grad_kw = jnp.einsum("jhqk,jqhd->jkhd", dscores, q4, preferred_element_type=jnp.float32)
    grad_vw = jnp.einsum("jhqk,jqhd->jkhd", rounded, up4, preferred_element_type=jnp.float32)
    grad_kvw = jnp.concatenate(
        [grad_kw.reshape(unit_count, window, head_cols), grad_vw.reshape(unit_count, window, head_cols)],
        axis=2,
    )
    total = jnp.zeros((near_rows, 2 * head_cols), jnp.float32)
    for j in range(unit_count):
        start = rel_starts[j] * UNIT
        total = lax.dynamic_update_slice_in_dim(
            total, lax.dynamic_slice_in_dim(total, start, window, 0) + grad_kvw[j], start, 0
        )
    return grad_q.reshape(rows, head_cols), normed, total


def per_device(heads_in, doc_units):
    section = lax.axis_index("sec")
    seq_place = lax.axis_index("seq")
    is_first = section == 0
    local_heads = heads_in[0]
    _, rows, cols = local_heads.shape
    half = cols // 2
    unit_count = rows // UNIT
    halo_units = MAX_DOC_UNITS - 1
    halo = halo_units * UNIT
    total_cols = cols * lax.axis_size("mp")
    chunks = 2 if (half // DH) % 2 == 0 else 1
    width = half // chunks

    keep_offset = section * half
    send_offset = (1 - section) * half
    rel_starts, allowed = window_plan(doc_units, seq_place, unit_count, halo_units)

    saved, partial = [], []
    for c in range(chunks):
        sent = lax.dynamic_slice_in_dim(local_heads, send_offset + c * width, width, 2)
        kept = lax.dynamic_slice_in_dim(local_heads, keep_offset + c * width, width, 2)
        arrived = sec_swap(sent)
        if partial:
            arrived, partial[-1] = lax.optimization_barrier((arrived, partial[-1]))
        key_value = jnp.where(is_first, kept, arrived)
        query_cot = jnp.where(is_first, arrived, kept)
        joined = jnp.concatenate([key_value[0], key_value[1]], axis=1)
        low = seq_shift(joined[rows - halo :], 1)
        high = seq_shift(joined[:halo], -1)
        near = jnp.concatenate([low, joined, high], axis=0)
        state, sums = chunk_forward(
            query_cot[0], query_cot[1], near[:, :width], near[:, width:], rel_starts, allowed
        )
        saved.append(state)
        partial.append(sums)
    sums = partial[0]
    for more in partial[1:]:
        sums = sums + more
    sums = sums + sec_swap(sums)
    sums = sums + lax.ppermute(sums, "mp", [(0, 1), (1, 0)])
    squares, crosses = sums[0], sums[1]
    spread = jnp.sqrt(squares / total_cols + epsilon)
    shared = crosses / total_cols / spread

    near_rows = rows + 2 * halo
    keep_parts, back_parts = [], []
    pending = None
    previous_total = None
    for c in range(chunks + 1):
        if c < chunks:
            state = saved[c]
            if previous_total is not None:
                state, previous_total = lax.optimization_barrier((state, previous_total))
                pending = (previous_total,) + pending[1:]
            grad_q, normed, total = chunk_backward(state, spread, shared, rel_starts, near_rows)
            from_left = seq_shift(total[near_rows - halo :], 1)
            from_right = seq_shift(total[:halo], -1)
        if pending is not None:
            p_total, p_left, p_right, p_grad_q, p_normed = pending
            if c < chunks:
                p_left, p_right, total = lax.optimization_barrier((p_left, p_right, total))
            own = p_total[halo : halo + rows]
            own = own.at[:halo].add(p_left)
            own = own.at[rows - halo :].add(p_right)
            kv_pair = jnp.stack([own[:, :width], own[:, width:]]).astype(jnp.bfloat16)
            qn_pair = jnp.stack([p_grad_q.astype(jnp.bfloat16), p_normed.astype(jnp.bfloat16)])
            keep_parts.append(jnp.where(is_first, kv_pair, qn_pair))
            back_parts.append(sec_swap(jnp.where(is_first, qn_pair, kv_pair)))
        if c < chunks:
            pending = (total, from_left, from_right, grad_q, normed)
            previous_total = total
    keep_pair = jnp.concatenate(keep_parts, axis=2)
    back = jnp.concatenate(back_parts, axis=2)
    result = jnp.where(
        is_first,
        jnp.concatenate([keep_pair, back], axis=2),
        jnp.concatenate([back, keep_pair], axis=2),
    )
    return result[None]


def solution(mesh):
    return jax.shard_map(
        per_device,
        mesh=mesh,
        in_specs=(P("sec", None, "seq", "mp"), P()),
        out_specs=P("sec", None, "seq", "mp"),
        check_vma=False,
    )
```

```python
import jax
import jax.numpy as jnp
from jax import lax
from jax.sharding import PartitionSpec as P

UNIT = 128
HEADS = 32
DH = 64
MAX_DOC_UNITS = 3


epsilon = 1e-06


def seq_shift(value, steps):
    count = lax.axis_size("seq")
    initial, last = (max(0, -steps), min(count, count - steps))
    return lax.ppermute(value, "seq", [(source, source + steps) for source in range(initial, last)])


def sec_swap(value):
    return lax.ppermute(value, "sec", [(0, 1), (1, 0)])


def window_plan(doc_units, seq_place, unit_count, halo_units):
    ends = jnp.cumsum(doc_units).astype(jnp.int32)
    first_unit = seq_place * unit_count
    query_units = first_unit + jnp.arange(unit_count, dtype=jnp.int32)

    def unit_doc(units):
        counted = jnp.sum((ends[None, :] <= units[:, None]).astype(jnp.int32), axis=1)
        return jnp.where(units < 0, jnp.int32(-1), counted)

    starts = jnp.max(
        jnp.where(ends[None, :] <= query_units[:, None], ends[None, :], 0), axis=1
    ).astype(jnp.int32)
    key_units = starts[:, None] + jnp.arange(MAX_DOC_UNITS, dtype=jnp.int32)[None, :]
    allowed = unit_doc(key_units.reshape(-1)).reshape(key_units.shape) == unit_doc(query_units)[:, None]
    return starts - (first_unit - halo_units), allowed


def attention_grads(queries, cotangent, near_keys, near_values, rel_starts, allowed, total_fn, total_cols):
    rows, head_cols = queries.shape
    heads = head_cols // DH
    unit_count = rows // UNIT
    window = MAX_DOC_UNITS * UNIT
    score_scale = DH ** (-0.5)

    def windows(near):
        pieces = [
            lax.dynamic_slice_in_dim(near, rel_starts[j] * UNIT, window, 0) for j in range(unit_count)
        ]
        return jnp.stack(pieces).reshape(unit_count, window, heads, DH)

    keys_w = windows(near_keys)
    values_w = windows(near_values)
    q4 = queries.reshape(unit_count, UNIT, heads, DH)
    cot_float = cotangent.astype(jnp.float32)

    mask = jnp.repeat(allowed, UNIT, axis=1)[:, None, None, :]
    scores = (
        jnp.einsum("jqhd,jkhd->jhqk", q4, keys_w, preferred_element_type=jnp.float32) * score_scale
    )
    scores = jnp.where(mask, scores, -jnp.inf)
    row_max = jnp.max(scores, axis=3, keepdims=True)
    expven = jnp.exp(scores - row_max)
    weights = expven / jnp.sum(expven, axis=3, keepdims=True)
    rounded = weights.astype(jnp.bfloat16)
    attended4 = jnp.einsum("jhqk,jkhd->jqhd", rounded, values_w, preferred_element_type=jnp.float32)
    attended = attended4.reshape(rows, head_cols)

    squares, crosses = total_fn(
        (jnp.sum(attended * attended, axis=1), jnp.sum(cot_float * attended, axis=1))
    )
    spread = jnp.sqrt(squares / total_cols + epsilon)
    normed = attended / spread[:, None]
    shared = crosses / total_cols / spread
    upstream = ((cot_float - normed * shared[:, None]) / spread[:, None]).astype(jnp.bfloat16)
    up4 = upstream.reshape(unit_count, UNIT, heads, DH)

    delta = jnp.sum(up4.astype(jnp.float32) * attended4, axis=3)
    delta = jnp.transpose(delta, (0, 2, 1))[..., None]
    dprobs = jnp.einsum("jqhd,jkhd->jhqk", up4, values_w, preferred_element_type=jnp.float32)
    dscores = (weights * (dprobs - delta) * score_scale).astype(jnp.bfloat16)
    grad_q = jnp.einsum("jhqk,jkhd->jqhd", dscores, keys_w, preferred_element_type=jnp.float32)
    grad_kw = jnp.einsum("jhqk,jqhd->jkhd", dscores, q4, preferred_element_type=jnp.float32)
    grad_vw = jnp.einsum("jhqk,jqhd->jkhd", rounded, up4, preferred_element_type=jnp.float32)
    grad_kvw = jnp.concatenate(
        [grad_kw.reshape(unit_count, window, head_cols), grad_vw.reshape(unit_count, window, head_cols)],
        axis=2,
    )
    near_rows = near_keys.shape[0]
    total = jnp.zeros((near_rows, 2 * head_cols), jnp.float32)
    for j in range(unit_count):
        start = rel_starts[j] * UNIT
        total = lax.dynamic_update_slice_in_dim(
            total, lax.dynamic_slice_in_dim(total, start, window, 0) + grad_kvw[j], start, 0
        )
    return grad_q.reshape(rows, head_cols), normed, total


def per_device(heads_in, doc_units):
    section = lax.axis_index("sec")
    seq_place = lax.axis_index("seq")
    is_first = section == 0
    local_heads = heads_in[0]
    _, rows, cols = local_heads.shape
    half = cols // 2
    unit_count = rows // UNIT
    halo_units = MAX_DOC_UNITS - 1
    halo = halo_units * UNIT
    total_cols = cols * lax.axis_size("mp")

    keep_offset = section * half
    send_offset = (1 - section) * half
    sent = lax.dynamic_slice_in_dim(local_heads, send_offset, half, 2)
    kept = lax.dynamic_slice_in_dim(local_heads, keep_offset, half, 2)
    arrived = sec_swap(sent)
    key_value = jnp.where(is_first, kept, arrived)
    query_cot = jnp.where(is_first, arrived, kept)

    joined = jnp.concatenate([key_value[0], key_value[1]], axis=1)
    low = seq_shift(joined[rows - halo :], 1)
    high = seq_shift(joined[:halo], -1)
    near = jnp.concatenate([low, joined, high], axis=0)

    rel_starts, allowed = window_plan(doc_units, seq_place, unit_count, halo_units)

    def row_total(sums_pair):
        sums = jnp.stack(sums_pair)
        sums = sums + sec_swap(sums)
        sums = sums + lax.ppermute(sums, "mp", [(0, 1), (1, 0)])
        return sums[0], sums[1]

    grad_q, normed, total = attention_grads(
        query_cot[0],
        query_cot[1],
        near[:, :half],
        near[:, half:],
        rel_starts,
        allowed,
        row_total,
        total_cols,
    )
    from_left = seq_shift(total[near.shape[0] - halo :], 1)
    from_right = seq_shift(total[:halo], -1)
    own = total[halo : halo + rows]
    own = own.at[:halo].add(from_left)
    own = own.at[rows - halo :].add(from_right)
    grad_k = own[:, :half].astype(jnp.bfloat16)
    grad_v = own[:, half:].astype(jnp.bfloat16)

    kv_pair = jnp.stack([grad_k, grad_v])
    qn_pair = jnp.stack([grad_q.astype(jnp.bfloat16), normed.astype(jnp.bfloat16)])
    keep_pair = jnp.where(is_first, kv_pair, qn_pair)
    back = sec_swap(jnp.where(is_first, qn_pair, kv_pair))
    result = jnp.where(
        is_first,
        jnp.concatenate([keep_pair, back], axis=2),
        jnp.concatenate([back, keep_pair], axis=2),
    )
    return result[None]


def solution(mesh):
    return jax.shard_map(
        per_device,
        mesh=mesh,
        in_specs=(P("sec", None, "seq", "mp"), P()),
        out_specs=P("sec", None, "seq", "mp"),
        check_vma=False,
    )
```

```python
import jax
import jax.numpy as jnp
from jax import lax
from jax.sharding import PartitionSpec as P

UNIT = 128
HEADS = 32
DH = 64
MAX_DOC_UNITS = 3


epsilon = 1e-06


def seq_shift(value, steps):
    count = lax.axis_size("seq")
    initial, last = (max(0, -steps), min(count, count - steps))
    return lax.ppermute(value, "seq", [(source, source + steps) for source in range(initial, last)])


def sec_swap(value):
    return lax.ppermute(value, "sec", [(0, 1), (1, 0)])


def window_plan(doc_units, seq_place, unit_count, halo_units):
    ends = jnp.cumsum(doc_units).astype(jnp.int32)
    first_unit = seq_place * unit_count
    query_units = first_unit + jnp.arange(unit_count, dtype=jnp.int32)

    def unit_doc(units):
        counted = jnp.sum((ends[None, :] <= units[:, None]).astype(jnp.int32), axis=1)
        return jnp.where(units < 0, jnp.int32(-1), counted)

    starts = jnp.max(
        jnp.where(ends[None, :] <= query_units[:, None], ends[None, :], 0), axis=1
    ).astype(jnp.int32)
    key_units = starts[:, None] + jnp.arange(MAX_DOC_UNITS, dtype=jnp.int32)[None, :]
    allowed = unit_doc(key_units.reshape(-1)).reshape(key_units.shape) == unit_doc(query_units)[:, None]
    return starts - (first_unit - halo_units), allowed


def attention_grads(queries, cotangent, near_keys, near_values, rel_starts, allowed, total_fn, total_cols):
    rows, head_cols = queries.shape
    heads = head_cols // DH
    unit_count = rows // UNIT
    window = MAX_DOC_UNITS * UNIT
    score_scale = DH ** (-0.5)

    def windows(near):
        pieces = [
            lax.dynamic_slice_in_dim(near, rel_starts[j] * UNIT, window, 0) for j in range(unit_count)
        ]
        return jnp.stack(pieces).reshape(unit_count, window, heads, DH)

    keys_w = windows(near_keys)
    values_w = windows(near_values)
    q4 = queries.reshape(unit_count, UNIT, heads, DH)
    cot_float = cotangent.astype(jnp.float32)

    mask = jnp.repeat(allowed, UNIT, axis=1)[:, None, None, :]
    scores = (
        jnp.einsum("jqhd,jkhd->jhqk", q4, keys_w, preferred_element_type=jnp.float32) * score_scale
    )
    scores = jnp.where(mask, scores, -jnp.inf)
    row_max = jnp.max(scores, axis=3, keepdims=True)
    expven = jnp.exp(scores - row_max)
    weights = expven / jnp.sum(expven, axis=3, keepdims=True)
    rounded = weights.astype(jnp.bfloat16)
    attended4 = jnp.einsum("jhqk,jkhd->jqhd", rounded, values_w, preferred_element_type=jnp.float32)
    attended = attended4.reshape(rows, head_cols)

    squares, crosses = total_fn(
        (jnp.sum(attended * attended, axis=1), jnp.sum(cot_float * attended, axis=1))
    )
    spread = jnp.sqrt(squares / total_cols + epsilon)
    normed = attended / spread[:, None]
    shared = crosses / total_cols / spread
    upstream = ((cot_float - normed * shared[:, None]) / spread[:, None]).astype(jnp.bfloat16)
    up4 = upstream.reshape(unit_count, UNIT, heads, DH)

    delta = jnp.sum(up4.astype(jnp.float32) * attended4, axis=3)
    delta = jnp.transpose(delta, (0, 2, 1))[..., None]
    dprobs = jnp.einsum("jqhd,jkhd->jhqk", up4, values_w, preferred_element_type=jnp.float32)
    dscores = (weights * (dprobs - delta) * score_scale).astype(jnp.bfloat16)
    grad_q = jnp.einsum("jhqk,jkhd->jqhd", dscores, keys_w, preferred_element_type=jnp.float32)
    grad_kw = jnp.einsum("jhqk,jqhd->jkhd", dscores, q4, preferred_element_type=jnp.float32)
    grad_vw = jnp.einsum("jhqk,jqhd->jkhd", rounded, up4, preferred_element_type=jnp.float32)
    grad_kvw = jnp.concatenate(
        [grad_kw.reshape(unit_count, window, head_cols), grad_vw.reshape(unit_count, window, head_cols)],
        axis=2,
    )
    near_rows = near_keys.shape[0]
    total = jnp.zeros((near_rows, 2 * head_cols), jnp.float32)
    for j in range(unit_count):
        start = rel_starts[j] * UNIT
        total = lax.dynamic_update_slice_in_dim(
            total, lax.dynamic_slice_in_dim(total, start, window, 0) + grad_kvw[j], start, 0
        )
    return grad_q.reshape(rows, head_cols), normed, total


def per_device(heads_in, doc_units):
    section = lax.axis_index("sec")
    seq_place = lax.axis_index("seq")
    is_first = section == 0
    local_heads = heads_in[0]
    _, rows, cols = local_heads.shape
    half = cols // 2
    unit_count = rows // UNIT
    halo_units = MAX_DOC_UNITS - 1
    halo = halo_units * UNIT
    total_cols = cols * lax.axis_size("mp")

    keep_offset = section * half
    send_offset = (1 - section) * half
    sent = lax.dynamic_slice_in_dim(local_heads, send_offset, half, 2)
    kept = lax.dynamic_slice_in_dim(local_heads, keep_offset, half, 2)
    arrived = sec_swap(sent)
    key_value = jnp.where(is_first, kept, arrived)
    query_cot = jnp.where(is_first, arrived, kept)

    joined = jnp.concatenate([key_value[0], key_value[1]], axis=1)
    low = seq_shift(joined[rows - halo :], 1)
    high = seq_shift(joined[:halo], -1)
    near = jnp.concatenate([low, joined, high], axis=0)

    rel_starts, allowed = window_plan(doc_units, seq_place, unit_count, halo_units)

    def row_total(sums_pair):
        sums = jnp.stack(sums_pair)
        sums = sums + sec_swap(sums)
        sums = sums + lax.ppermute(sums, "mp", [(0, 1), (1, 0)])
        return sums[0], sums[1]

    grad_q, normed, total = attention_grads(
        query_cot[0],
        query_cot[1],
        near[:, :half],
        near[:, half:],
        rel_starts,
        allowed,
        row_total,
        total_cols,
    )
    from_left = seq_shift(total[near.shape[0] - halo :].astype(jnp.bfloat16), 1)
    from_right = seq_shift(total[:halo].astype(jnp.bfloat16), -1)
    own = (
        total[halo : halo + rows]
        + jnp.pad(from_left.astype(jnp.float32), ((0, rows - halo), (0, 0)))
        + jnp.pad(from_right.astype(jnp.float32), ((rows - halo, 0), (0, 0)))
    )
    grad_k = own[:, :half].astype(jnp.bfloat16)
    grad_v = own[:, half:].astype(jnp.bfloat16)

    kv_pair = jnp.stack([grad_k, grad_v])
    qn_pair = jnp.stack([grad_q.astype(jnp.bfloat16), normed.astype(jnp.bfloat16)])
    keep_pair = jnp.where(is_first, kv_pair, qn_pair)
    back = sec_swap(jnp.where(is_first, qn_pair, kv_pair))
    result = jnp.where(
        is_first,
        jnp.concatenate([keep_pair, back], axis=2),
        jnp.concatenate([back, keep_pair], axis=2),
    )
    return result[None]


def solution(mesh):
    return jax.shard_map(
        per_device,
        mesh=mesh,
        in_specs=(P("sec", None, "seq", "mp"), P()),
        out_specs=P("sec", None, "seq", "mp"),
        check_vma=False,
    )
```

```python
import jax
import jax.numpy as jnp
from jax import lax
from jax.experimental import pallas as pl
from jax.experimental.pallas import tpu as pltpu
from jax.sharding import PartitionSpec as P

UNIT = 128
HEADS = 32
DH = 64
MAX_DOC_UNITS = 3


epsilon = 1e-06


def seq_shift(value, steps):
    count = lax.axis_size("seq")
    initial, last = (max(0, -steps), min(count, count - steps))
    return lax.ppermute(value, "seq", [(source, source + steps) for source in range(initial, last)])


def sec_swap(value):
    return lax.ppermute(value, "sec", [(0, 1), (1, 0)])


def window_plan(doc_units, seq_place, unit_count, halo_units):
    ends = jnp.cumsum(doc_units).astype(jnp.int32)
    first_unit = seq_place * unit_count
    query_units = first_unit + jnp.arange(unit_count, dtype=jnp.int32)

    def unit_doc(units):
        counted = jnp.sum((ends[None, :] <= units[:, None]).astype(jnp.int32), axis=1)
        return jnp.where(units < 0, jnp.int32(-1), counted)

    starts = jnp.max(
        jnp.where(ends[None, :] <= query_units[:, None], ends[None, :], 0), axis=1
    ).astype(jnp.int32)
    key_units = starts[:, None] + jnp.arange(MAX_DOC_UNITS, dtype=jnp.int32)[None, :]
    allowed = unit_doc(key_units.reshape(-1)).reshape(key_units.shape) == unit_doc(query_units)[:, None]
    near_units = unit_count + 2 * halo_units
    rel_starts = jnp.clip(starts - (first_unit - halo_units), 0, near_units - MAX_DOC_UNITS)
    return rel_starts, allowed


PAIR = 2 * DH


def pair_softmax(q_pair, k_pair, mask, lane_low):
    score_scale = DH ** (-0.5)
    result = []
    for chosen in (lane_low, jnp.logical_not(lane_low)):
        q_one = jnp.where(chosen, q_pair, jnp.zeros_like(q_pair))
        scores = (
            lax.dot_general(q_one, k_pair, (((1,), (1,)), ((), ())), preferred_element_type=jnp.float32)
            * score_scale
        )
        scores = jnp.where(mask, scores, -jnp.inf)
        row_max = jnp.max(scores, axis=1, keepdims=True)
        expven = jnp.exp(scores - row_max)
        result.append((chosen, expven / jnp.sum(expven, axis=1, keepdims=True)))
    return result


def window_mask(allow_ref, j):
    window = MAX_DOC_UNITS * UNIT
    block = lax.broadcasted_iota(jnp.int32, (UNIT, window), 1) // UNIT
    mask = jnp.zeros((UNIT, window), jnp.bool_)
    for w in range(MAX_DOC_UNITS):
        mask = jnp.logical_or(mask, jnp.logical_and(block == w, allow_ref[j * MAX_DOC_UNITS + w] != 0))
    return mask


def forward_kernel(rel_ref, allow_ref, q_ref, kv_ref, out_ref):
    rows, head_cols = q_ref.shape
    window = MAX_DOC_UNITS * UNIT
    lane_low = lax.broadcasted_iota(jnp.int32, (UNIT, PAIR), 1) < DH
    for j in range(rows // UNIT):
        start = pl.multiple_of(rel_ref[j] * UNIT, UNIT)
        mask = window_mask(allow_ref, j)
        for p in range(head_cols // PAIR):
            q_pair = q_ref[pl.ds(j * UNIT, UNIT), pl.ds(p * PAIR, PAIR)]
            k_pair = kv_ref[pl.ds(start, window), pl.ds(p * PAIR, PAIR)]
            v_pair = kv_ref[pl.ds(start, window), pl.ds(head_cols + p * PAIR, PAIR)]
            outs = [
                jnp.dot(weights.astype(jnp.bfloat16), v_pair, preferred_element_type=jnp.float32)
                for _, weights in pair_softmax(q_pair, k_pair, mask, lane_low)
            ]
            out_ref[pl.ds(j * UNIT, UNIT), pl.ds(p * PAIR, PAIR)] = jnp.where(lane_low, outs[0], outs[1])


def backward_kernel(rel_ref, allow_ref, q_ref, up_ref, att_ref, kv_ref, dq_ref, dkv_ref):
    rows, head_cols = q_ref.shape
    window = MAX_DOC_UNITS * UNIT
    score_scale = DH ** (-0.5)
    lane_low = lax.broadcasted_iota(jnp.int32, (UNIT, PAIR), 1) < DH
    wide_low = lax.broadcasted_iota(jnp.int32, (window, PAIR), 1) < DH
    dkv_ref[...] = jnp.zeros(dkv_ref.shape, dkv_ref.dtype)
    contract_rows = (((0,), (0,)), ((), ()))
    for j in range(rows // UNIT):
        start = pl.multiple_of(rel_ref[j] * UNIT, UNIT)
        mask = window_mask(allow_ref, j)
        for p in range(head_cols // PAIR):
            q_pair = q_ref[pl.ds(j * UNIT, UNIT), pl.ds(p * PAIR, PAIR)]
            up_pair = up_ref[pl.ds(j * UNIT, UNIT), pl.ds(p * PAIR, PAIR)]
            att_pair = att_ref[pl.ds(j * UNIT, UNIT), pl.ds(p * PAIR, PAIR)]
            k_pair = kv_ref[pl.ds(start, window), pl.ds(p * PAIR, PAIR)]
            v_pair = kv_ref[pl.ds(start, window), pl.ds(head_cols + p * PAIR, PAIR)]
            product = up_pair.astype(jnp.float32) * att_pair
            grads = []
            for chosen, weights in pair_softmax(q_pair, k_pair, mask, lane_low):
                delta = jnp.sum(jnp.where(chosen, product, 0.0), axis=1, keepdims=True)
                up_one = jnp.where(chosen, up_pair, jnp.zeros_like(up_pair))
                dprobs = lax.dot_general(
                    up_one, v_pair, (((1,), (1,)), ((), ())), preferred_element_type=jnp.float32
                )
                dscores = (weights * (dprobs - delta) * score_scale).astype(jnp.bfloat16)
                grads.append(
                    (
                        jnp.dot(dscores, k_pair, preferred_element_type=jnp.float32),
                        lax.dot_general(dscores, q_pair, contract_rows, preferred_element_type=jnp.float32),
                        lax.dot_general(
                            weights.astype(jnp.bfloat16), up_pair, contract_rows,
                            preferred_element_type=jnp.float32,
                        ),
                    )
                )
            (dq_a, dk_a, dv_a), (dq_b, dk_b, dv_b) = grads
            dq_ref[pl.ds(j * UNIT, UNIT), pl.ds(p * PAIR, PAIR)] = jnp.where(lane_low, dq_a, dq_b)
            k_rows = (pl.ds(start, window), pl.ds(p * PAIR, PAIR))
            v_rows = (pl.ds(start, window), pl.ds(head_cols + p * PAIR, PAIR))
            dkv_ref[k_rows] = dkv_ref[k_rows] + jnp.where(wide_low, dk_a, dk_b)
            dkv_ref[v_rows] = dkv_ref[v_rows] + jnp.where(wide_low, dv_a, dv_b)


def whole_call(kernel, scalars, arrays, outs):
    def spec(shape):
        return pl.BlockSpec(shape, lambda i, *_: (0,) * len(shape))

    return pl.pallas_call(
        kernel,
        grid_spec=pltpu.PrefetchScalarGridSpec(
            num_scalar_prefetch=len(scalars),
            grid=(1,),
            in_specs=[spec(a.shape) for a in arrays],
            out_specs=[spec(o.shape) for o in outs],
        ),
        out_shape=outs,
    )(*scalars, *arrays)


def attention_grads(queries, cotangent, near, rel_starts, allowed, total_fn, total_cols):
    rows, head_cols = queries.shape
    near_rows = near.shape[0]
    allow_flat = allowed.reshape(-1).astype(jnp.int32)
    scalars = (rel_starts.astype(jnp.int32), allow_flat)
    (attended,) = whole_call(
        forward_kernel, scalars, (queries, near), [jax.ShapeDtypeStruct((rows, head_cols), jnp.float32)]
    )
    cot_float = cotangent.astype(jnp.float32)
    squares, crosses = total_fn(
        (jnp.sum(attended * attended, axis=1), jnp.sum(cot_float * attended, axis=1))
    )
    spread = jnp.sqrt(squares / total_cols + epsilon)
    normed = attended / spread[:, None]
    shared = crosses / total_cols / spread
    upstream = ((cot_float - normed * shared[:, None]) / spread[:, None]).astype(jnp.bfloat16)
    grad_q, total = whole_call(
        backward_kernel,
        scalars,
        (queries, upstream, attended, near),
        [
            jax.ShapeDtypeStruct((rows, head_cols), jnp.float32),
            jax.ShapeDtypeStruct((near_rows, 2 * head_cols), jnp.float32),
        ],
    )
    return grad_q, normed, total


def per_device(heads_in, doc_units):
    section = lax.axis_index("sec")
    seq_place = lax.axis_index("seq")
    is_first = section == 0
    local_heads = heads_in[0]
    _, rows, cols = local_heads.shape
    half = cols // 2
    unit_count = rows // UNIT
    halo_units = MAX_DOC_UNITS - 1
    halo = halo_units * UNIT
    total_cols = cols * lax.axis_size("mp")

    keep_offset = section * half
    send_offset = (1 - section) * half
    sent = lax.dynamic_slice_in_dim(local_heads, send_offset, half, 2)
    kept = lax.dynamic_slice_in_dim(local_heads, keep_offset, half, 2)
    arrived = sec_swap(sent)
    key_value = jnp.where(is_first, kept, arrived)
    query_cot = jnp.where(is_first, arrived, kept)

    joined = jnp.concatenate([key_value[0], key_value[1]], axis=1)
    low = seq_shift(joined[rows - halo :], 1)
    high = seq_shift(joined[:halo], -1)
    near = jnp.concatenate([low, joined, high], axis=0)

    rel_starts, allowed = window_plan(doc_units, seq_place, unit_count, halo_units)

    def row_total(sums_pair):
        sums = jnp.stack(sums_pair)
        sums = sums + sec_swap(sums)
        sums = sums + lax.ppermute(sums, "mp", [(0, 1), (1, 0)])
        return sums[0], sums[1]

    grad_q, normed, total = attention_grads(
        query_cot[0],
        query_cot[1],
        near,
        rel_starts,
        allowed,
        row_total,
        total_cols,
    )
    from_left = seq_shift(total[near.shape[0] - halo :].astype(jnp.bfloat16), 1)
    from_right = seq_shift(total[:halo].astype(jnp.bfloat16), -1)
    own = (
        total[halo : halo + rows]
        + jnp.pad(from_left.astype(jnp.float32), ((0, rows - halo), (0, 0)))
        + jnp.pad(from_right.astype(jnp.float32), ((rows - halo, 0), (0, 0)))
    )
    grad_k = own[:, :half].astype(jnp.bfloat16)
    grad_v = own[:, half:].astype(jnp.bfloat16)

    kv_pair = jnp.stack([grad_k, grad_v])
    qn_pair = jnp.stack([grad_q.astype(jnp.bfloat16), normed.astype(jnp.bfloat16)])
    keep_pair = jnp.where(is_first, kv_pair, qn_pair)
    back = sec_swap(jnp.where(is_first, qn_pair, kv_pair))
    result = jnp.where(
        is_first,
        jnp.concatenate([keep_pair, back], axis=2),
        jnp.concatenate([back, keep_pair], axis=2),
    )
    return result[None]


def solution(mesh):
    return jax.shard_map(
        per_device,
        mesh=mesh,
        in_specs=(P("sec", None, "seq", "mp"), P()),
        out_specs=P("sec", None, "seq", "mp"),
        check_vma=False,
    )
```

```python
import jax
import jax.numpy as jnp
from jax import lax
from jax.sharding import PartitionSpec as P

UNIT = 128
HEADS = 32
DH = 64
MAX_DOC_UNITS = 3


epsilon = 1e-06


def seq_shift(value, steps):
    count = lax.axis_size("seq")
    initial, last = (max(0, -steps), min(count, count - steps))
    return lax.ppermute(value, "seq", [(source, source + steps) for source in range(initial, last)])


def sec_swap(value):
    return lax.ppermute(value, "sec", [(0, 1), (1, 0)])


def window_plan(doc_units, seq_place, unit_count, halo_units):
    ends = jnp.cumsum(doc_units).astype(jnp.int32)
    first_unit = seq_place * unit_count
    query_units = first_unit + jnp.arange(unit_count, dtype=jnp.int32)

    def unit_doc(units):
        counted = jnp.sum((ends[None, :] <= units[:, None]).astype(jnp.int32), axis=1)
        return jnp.where(units < 0, jnp.int32(-1), counted)

    starts = jnp.max(
        jnp.where(ends[None, :] <= query_units[:, None], ends[None, :], 0), axis=1
    ).astype(jnp.int32)
    key_units = starts[:, None] + jnp.arange(MAX_DOC_UNITS, dtype=jnp.int32)[None, :]
    allowed = unit_doc(key_units.reshape(-1)).reshape(key_units.shape) == unit_doc(query_units)[:, None]
    return starts - (first_unit - halo_units), allowed


def attention_grads(queries, cotangent, near_keys, near_values, rel_starts, allowed, total_fn, total_cols):
    rows, head_cols = queries.shape
    heads = head_cols // DH
    unit_count = rows // UNIT
    window = MAX_DOC_UNITS * UNIT
    score_scale = DH ** (-0.5)

    def windows(near):
        pieces = [
            lax.dynamic_slice_in_dim(near, rel_starts[j] * UNIT, window, 0) for j in range(unit_count)
        ]
        return jnp.stack(pieces).reshape(unit_count, window, heads, DH)

    keys_w = windows(near_keys)
    values_w = windows(near_values)
    q4 = queries.reshape(unit_count, UNIT, heads, DH)
    cot_float = cotangent.astype(jnp.float32)

    mask = jnp.repeat(allowed, UNIT, axis=1)[:, None, None, :]
    scores = (
        jnp.einsum("jqhd,jkhd->jhqk", q4, keys_w, preferred_element_type=jnp.float32) * score_scale
    )
    scores = jnp.where(mask, scores, -jnp.inf)
    row_max = jnp.max(scores, axis=3, keepdims=True)
    expven = jnp.exp(scores - row_max)
    weights = expven / jnp.sum(expven, axis=3, keepdims=True)
    rounded = weights.astype(jnp.bfloat16)
    attended4 = jnp.einsum("jhqk,jkhd->jqhd", rounded, values_w, preferred_element_type=jnp.float32)
    attended = attended4.reshape(rows, head_cols)

    squares, crosses = total_fn(
        (jnp.sum(attended * attended, axis=1), jnp.sum(cot_float * attended, axis=1))
    )
    spread = jnp.sqrt(squares / total_cols + epsilon)
    normed = attended / spread[:, None]
    shared = crosses / total_cols / spread
    upstream = ((cot_float - normed * shared[:, None]) / spread[:, None]).astype(jnp.bfloat16)
    up4 = upstream.reshape(unit_count, UNIT, heads, DH)

    delta = jnp.sum(up4.astype(jnp.float32) * attended4, axis=3)
    delta = jnp.transpose(delta, (0, 2, 1))[..., None]
    dprobs = jnp.einsum("jqhd,jkhd->jhqk", up4, values_w, preferred_element_type=jnp.float32)
    dscores = (weights * (dprobs - delta) * score_scale).astype(jnp.bfloat16)
    grad_q = jnp.einsum("jhqk,jkhd->jqhd", dscores, keys_w, preferred_element_type=jnp.float32)
    grad_kw = jnp.einsum("jhqk,jqhd->jkhd", dscores, q4, preferred_element_type=jnp.float32)
    grad_vw = jnp.einsum("jhqk,jqhd->jkhd", rounded, up4, preferred_element_type=jnp.float32)
    grad_kvw = jnp.concatenate(
        [grad_kw.reshape(unit_count, window, head_cols), grad_vw.reshape(unit_count, window, head_cols)],
        axis=2,
    )
    near_rows = near_keys.shape[0]
    total = jnp.zeros((near_rows, 2 * head_cols), jnp.float32)
    for j in range(unit_count):
        start = rel_starts[j] * UNIT
        total = lax.dynamic_update_slice_in_dim(
            total, lax.dynamic_slice_in_dim(total, start, window, 0) + grad_kvw[j], start, 0
        )
    return grad_q.reshape(rows, head_cols), normed, total


def per_device(heads_in, doc_units):
    section = lax.axis_index("sec")
    seq_place = lax.axis_index("seq")
    is_first = section == 0
    local_heads = heads_in[0]
    _, rows, cols = local_heads.shape
    half = cols // 2
    unit_count = rows // UNIT
    halo_units = MAX_DOC_UNITS - 1
    halo = halo_units * UNIT
    total_cols = cols * lax.axis_size("mp")

    keep_offset = section * half
    send_offset = (1 - section) * half
    sent = lax.dynamic_slice_in_dim(local_heads, send_offset, half, 2)
    kept = lax.dynamic_slice_in_dim(local_heads, keep_offset, half, 2)
    arrived = sec_swap(sent)
    key_value = jnp.where(is_first, kept, arrived)
    query_cot = jnp.where(is_first, arrived, kept)

    joined = jnp.concatenate([key_value[0], key_value[1]], axis=1)
    low = seq_shift(joined[rows - halo :], 1)
    high = seq_shift(joined[:halo], -1)
    near = jnp.concatenate([low, joined, high], axis=0)

    rel_starts, allowed = window_plan(doc_units, seq_place, unit_count, halo_units)

    def row_total(sums_pair):
        gathered = lax.all_gather(jnp.stack(sums_pair), ("sec", "mp"))
        sums = gathered[0]
        for more in range(1, gathered.shape[0]):
            sums = sums + gathered[more]
        return sums[0], sums[1]

    grad_q, normed, total = attention_grads(
        query_cot[0],
        query_cot[1],
        near[:, :half],
        near[:, half:],
        rel_starts,
        allowed,
        row_total,
        total_cols,
    )
    from_left = seq_shift(total[near.shape[0] - halo :].astype(jnp.bfloat16), 1)
    from_right = seq_shift(total[:halo].astype(jnp.bfloat16), -1)
    own = (
        total[halo : halo + rows]
        + jnp.pad(from_left.astype(jnp.float32), ((0, rows - halo), (0, 0)))
        + jnp.pad(from_right.astype(jnp.float32), ((rows - halo, 0), (0, 0)))
    )
    grad_k = own[:, :half].astype(jnp.bfloat16)
    grad_v = own[:, half:].astype(jnp.bfloat16)

    kv_pair = jnp.stack([grad_k, grad_v])
    qn_pair = jnp.stack([grad_q.astype(jnp.bfloat16), normed.astype(jnp.bfloat16)])
    keep_pair = jnp.where(is_first, kv_pair, qn_pair)
    back = sec_swap(jnp.where(is_first, qn_pair, kv_pair))
    result = jnp.where(
        is_first,
        jnp.concatenate([keep_pair, back], axis=2),
        jnp.concatenate([back, keep_pair], axis=2),
    )
    return result[None]


def solution(mesh):
    return jax.shard_map(
        per_device,
        mesh=mesh,
        in_specs=(P("sec", None, "seq", "mp"), P()),
        out_specs=P("sec", None, "seq", "mp"),
        check_vma=False,
    )
```

```python
import jax
import jax.numpy as jnp
from jax import lax
from jax.experimental.layout import Layout, with_layout_constraint
from jax.sharding import PartitionSpec as P

UNIT = 128
HEADS = 32
DH = 64
MAX_DOC_UNITS = 3


epsilon = 1e-06


def seq_shift(value, steps):
    count = lax.axis_size("seq")
    initial, last = (max(0, -steps), min(count, count - steps))
    return lax.ppermute(value, "seq", [(source, source + steps) for source in range(initial, last)])


def sec_swap(value):
    return lax.ppermute(value, "sec", [(0, 1), (1, 0)])


def window_plan(doc_units, seq_place, unit_count, halo_units):
    ends = jnp.cumsum(doc_units).astype(jnp.int32)
    first_unit = seq_place * unit_count
    query_units = first_unit + jnp.arange(unit_count, dtype=jnp.int32)

    def unit_doc(units):
        counted = jnp.sum((ends[None, :] <= units[:, None]).astype(jnp.int32), axis=1)
        return jnp.where(units < 0, jnp.int32(-1), counted)

    starts = jnp.max(
        jnp.where(ends[None, :] <= query_units[:, None], ends[None, :], 0), axis=1
    ).astype(jnp.int32)
    key_units = starts[:, None] + jnp.arange(MAX_DOC_UNITS, dtype=jnp.int32)[None, :]
    allowed = unit_doc(key_units.reshape(-1)).reshape(key_units.shape) == unit_doc(query_units)[:, None]
    return starts - (first_unit - halo_units), allowed


def attention_grads(queries, cotangent, near_keys, near_values, rel_starts, allowed, total_fn, total_cols):
    rows, head_cols = queries.shape
    heads = head_cols // DH
    unit_count = rows // UNIT
    window = MAX_DOC_UNITS * UNIT
    score_scale = DH ** (-0.5)

    def windows(near):
        pieces = [
            lax.dynamic_slice_in_dim(near, rel_starts[j] * UNIT, window, 0) for j in range(unit_count)
        ]
        return jnp.stack(pieces).reshape(unit_count, window, heads, DH)

    keys_w = windows(near_keys)
    values_w = windows(near_values)
    q4 = queries.reshape(unit_count, UNIT, heads, DH)
    cot_float = cotangent.astype(jnp.float32)

    mask = jnp.repeat(allowed, UNIT, axis=1)[:, None, None, :]
    scores = (
        jnp.einsum("jqhd,jkhd->jhqk", q4, keys_w, preferred_element_type=jnp.float32) * score_scale
    )
    scores = jnp.where(mask, scores, -jnp.inf)
    row_max = jnp.max(scores, axis=3, keepdims=True)
    expven = jnp.exp(scores - row_max)
    weights = expven / jnp.sum(expven, axis=3, keepdims=True)
    rounded = weights.astype(jnp.bfloat16)
    attended4 = jnp.einsum("jhqk,jkhd->jqhd", rounded, values_w, preferred_element_type=jnp.float32)
    attended = attended4.reshape(rows, head_cols)

    squares, crosses = total_fn(
        (jnp.sum(attended * attended, axis=1), jnp.sum(cot_float * attended, axis=1))
    )
    spread = jnp.sqrt(squares / total_cols + epsilon)
    normed = attended / spread[:, None]
    shared = crosses / total_cols / spread
    upstream = ((cot_float - normed * shared[:, None]) / spread[:, None]).astype(jnp.bfloat16)
    up4 = upstream.reshape(unit_count, UNIT, heads, DH)

    delta = jnp.sum(up4.astype(jnp.float32) * attended4, axis=3)
    delta = jnp.transpose(delta, (0, 2, 1))[..., None]
    dprobs = jnp.einsum("jqhd,jkhd->jhqk", up4, values_w, preferred_element_type=jnp.float32)
    dscores = (weights * (dprobs - delta) * score_scale).astype(jnp.bfloat16)
    grad_q = jnp.einsum("jhqk,jkhd->jqhd", dscores, keys_w, preferred_element_type=jnp.float32)
    grad_kw = jnp.einsum("jhqk,jqhd->jkhd", dscores, q4, preferred_element_type=jnp.float32)
    grad_vw = jnp.einsum("jhqk,jqhd->jkhd", rounded, up4, preferred_element_type=jnp.float32)
    grad_kvw = jnp.concatenate(
        [grad_kw.reshape(unit_count, window, head_cols), grad_vw.reshape(unit_count, window, head_cols)],
        axis=2,
    )
    near_rows = near_keys.shape[0]
    total = jnp.zeros((near_rows, 2 * head_cols), jnp.float32)
    for j in range(unit_count):
        start = rel_starts[j] * UNIT
        total = lax.dynamic_update_slice_in_dim(
            total, lax.dynamic_slice_in_dim(total, start, window, 0) + grad_kvw[j], start, 0
        )
    return grad_q.reshape(rows, head_cols), normed, total


def per_device(heads_in, doc_units):
    section = lax.axis_index("sec")
    seq_place = lax.axis_index("seq")
    is_first = section == 0
    local_heads = heads_in[0]
    _, rows, cols = local_heads.shape
    half = cols // 2
    unit_count = rows // UNIT
    halo_units = MAX_DOC_UNITS - 1
    halo = halo_units * UNIT
    total_cols = cols * lax.axis_size("mp")

    keep_offset = section * half
    send_offset = (1 - section) * half
    sent = lax.dynamic_slice_in_dim(local_heads, send_offset, half, 2)
    kept = lax.dynamic_slice_in_dim(local_heads, keep_offset, half, 2)
    arrived = sec_swap(sent)
    key_value = jnp.where(is_first, kept, arrived)
    query_cot = jnp.where(is_first, arrived, kept)

    joined = jnp.concatenate([key_value[0], key_value[1]], axis=1)
    low = seq_shift(joined[rows - halo :], 1)
    high = seq_shift(joined[:halo], -1)
    near = jnp.concatenate([low, joined, high], axis=0)

    rel_starts, allowed = window_plan(doc_units, seq_place, unit_count, halo_units)

    def row_total(sums_pair):
        sums = jnp.stack(sums_pair)
        sums = sums + sec_swap(sums)
        sums = sums + lax.ppermute(sums, "mp", [(0, 1), (1, 0)])
        return sums[0], sums[1]

    grad_q, normed, total = attention_grads(
        query_cot[0],
        query_cot[1],
        near[:, :half],
        near[:, half:],
        rel_starts,
        allowed,
        row_total,
        total_cols,
    )
    from_left = seq_shift(total[near.shape[0] - halo :].astype(jnp.bfloat16), 1)
    from_right = seq_shift(total[:halo].astype(jnp.bfloat16), -1)
    own = (
        total[halo : halo + rows]
        + jnp.pad(from_left.astype(jnp.float32), ((0, rows - halo), (0, 0)))
        + jnp.pad(from_right.astype(jnp.float32), ((rows - halo, 0), (0, 0)))
    )
    grad_k = own[:, :half].astype(jnp.bfloat16)
    grad_v = own[:, half:].astype(jnp.bfloat16)

    kv_pair = jnp.stack([grad_k, grad_v])
    qn_pair = jnp.stack([grad_q.astype(jnp.bfloat16), normed.astype(jnp.bfloat16)])
    keep_pair = jnp.where(is_first, kv_pair, qn_pair)
    leaving = with_layout_constraint(jnp.where(is_first, qn_pair, kv_pair), Layout((0, 1, 2)))
    keep_pair = with_layout_constraint(keep_pair, Layout((0, 1, 2)))
    back = sec_swap(leaving)
    result = jnp.where(
        is_first,
        jnp.concatenate([keep_pair, back], axis=2),
        jnp.concatenate([back, keep_pair], axis=2),
    )
    return result[None]


def solution(mesh):
    return jax.shard_map(
        per_device,
        mesh=mesh,
        in_specs=(P("sec", None, "seq", "mp"), P()),
        out_specs=P("sec", None, "seq", "mp"),
        check_vma=False,
    )
```

```python
import jax
import jax.numpy as jnp
from jax import lax
from jax.sharding import PartitionSpec as P

UNIT = 128
HEADS = 32
DH = 64
MAX_DOC_UNITS = 3


epsilon = 1e-06


def seq_shift(value, steps):
    count = lax.axis_size("seq")
    initial, last = (max(0, -steps), min(count, count - steps))
    return lax.ppermute(value, "seq", [(source, source + steps) for source in range(initial, last)])


def sec_swap(value):
    return lax.ppermute(value, "sec", [(0, 1), (1, 0)])


def window_plan(doc_units, seq_place, unit_count, halo_units):
    ends = jnp.cumsum(doc_units).astype(jnp.int32)
    first_unit = seq_place * unit_count
    query_units = first_unit + jnp.arange(unit_count, dtype=jnp.int32)

    def unit_doc(units):
        counted = jnp.sum((ends[None, :] <= units[:, None]).astype(jnp.int32), axis=1)
        return jnp.where(units < 0, jnp.int32(-1), counted)

    starts = jnp.max(
        jnp.where(ends[None, :] <= query_units[:, None], ends[None, :], 0), axis=1
    ).astype(jnp.int32)
    key_units = starts[:, None] + jnp.arange(MAX_DOC_UNITS, dtype=jnp.int32)[None, :]
    allowed = unit_doc(key_units.reshape(-1)).reshape(key_units.shape) == unit_doc(query_units)[:, None]
    return starts - (first_unit - halo_units), allowed


def attention_grads(queries, cotangent, near_keys, near_values, rel_starts, allowed, total_fn, total_cols):
    rows, head_cols = queries.shape
    heads = head_cols // DH
    unit_count = rows // UNIT
    window = MAX_DOC_UNITS * UNIT
    score_scale = DH ** (-0.5)

    def windows(near):
        pieces = [
            lax.dynamic_slice_in_dim(near, rel_starts[j] * UNIT, window, 0) for j in range(unit_count)
        ]
        return jnp.stack(pieces).reshape(unit_count, window, heads, DH)

    keys_w = windows(near_keys)
    values_w = windows(near_values)
    q4 = queries.reshape(unit_count, UNIT, heads, DH)
    cot_float = cotangent.astype(jnp.float32)

    mask = jnp.repeat(allowed, UNIT, axis=1)[:, None, None, :]
    scores = (
        jnp.einsum("jqhd,jkhd->jhqk", q4, keys_w, preferred_element_type=jnp.float32) * score_scale
    )
    scores = jnp.where(mask, scores, -jnp.inf)
    row_max = jnp.max(scores, axis=3, keepdims=True)
    expven = jnp.exp(scores - row_max)
    weights = expven / jnp.sum(expven, axis=3, keepdims=True)
    rounded = weights.astype(jnp.bfloat16)
    attended4 = jnp.einsum("jhqk,jkhd->jqhd", rounded, values_w, preferred_element_type=jnp.float32)
    attended = attended4.reshape(rows, head_cols)

    squares, crosses = total_fn(
        (jnp.sum(attended * attended, axis=1), jnp.sum(cot_float * attended, axis=1))
    )
    spread = jnp.sqrt(squares / total_cols + epsilon)
    normed = attended / spread[:, None]
    shared = crosses / total_cols / spread
    upstream = ((cot_float - normed * shared[:, None]) / spread[:, None]).astype(jnp.bfloat16)
    up4 = upstream.reshape(unit_count, UNIT, heads, DH)

    delta = jnp.sum(up4.astype(jnp.float32) * attended4, axis=3)
    delta = jnp.transpose(delta, (0, 2, 1))[..., None]
    dprobs = jnp.einsum("jqhd,jkhd->jhqk", up4, values_w, preferred_element_type=jnp.float32)
    dscores = (weights * (dprobs - delta) * score_scale).astype(jnp.bfloat16)
    grad_kw = jnp.einsum("jhqk,jqhd->jkhd", dscores, q4, preferred_element_type=jnp.float32)
    grad_vw = jnp.einsum("jhqk,jqhd->jkhd", rounded, up4, preferred_element_type=jnp.float32)
    grad_kvw = jnp.concatenate(
        [grad_kw.reshape(unit_count, window, head_cols), grad_vw.reshape(unit_count, window, head_cols)],
        axis=2,
    )
    near_rows = near_keys.shape[0]
    total = jnp.zeros((near_rows, 2 * head_cols), jnp.float32)
    for j in range(unit_count):
        start = rel_starts[j] * UNIT
        total = lax.dynamic_update_slice_in_dim(
            total, lax.dynamic_slice_in_dim(total, start, window, 0) + grad_kvw[j], start, 0
        )
    return (dscores, keys_w), normed, total


def per_device(heads_in, doc_units):
    section = lax.axis_index("sec")
    seq_place = lax.axis_index("seq")
    is_first = section == 0
    local_heads = heads_in[0]
    _, rows, cols = local_heads.shape
    half = cols // 2
    unit_count = rows // UNIT
    halo_units = MAX_DOC_UNITS - 1
    halo = halo_units * UNIT
    total_cols = cols * lax.axis_size("mp")

    keep_offset = section * half
    send_offset = (1 - section) * half
    sent = lax.dynamic_slice_in_dim(local_heads, send_offset, half, 2)
    kept = lax.dynamic_slice_in_dim(local_heads, keep_offset, half, 2)
    arrived = sec_swap(sent)
    key_value = jnp.where(is_first, kept, arrived)
    query_cot = jnp.where(is_first, arrived, kept)

    joined = jnp.concatenate([key_value[0], key_value[1]], axis=1)
    low = seq_shift(joined[rows - halo :], 1)
    high = seq_shift(joined[:halo], -1)
    near = jnp.concatenate([low, joined, high], axis=0)

    rel_starts, allowed = window_plan(doc_units, seq_place, unit_count, halo_units)

    def row_total(sums_pair):
        sums = jnp.stack(sums_pair)
        sums = sums + sec_swap(sums)
        sums = sums + lax.ppermute(sums, "mp", [(0, 1), (1, 0)])
        return sums[0], sums[1]

    grad_q, normed, total = attention_grads(
        query_cot[0],
        query_cot[1],
        near[:, :half],
        near[:, half:],
        rel_starts,
        allowed,
        row_total,
        total_cols,
    )
    to_left = total[near.shape[0] - halo :]
    to_right = total[:halo]
    dscores, keys_w, to_left, to_right = lax.optimization_barrier((*grad_q, to_left, to_right))
    grad_q = jnp.einsum(
        "jhqk,jkhd->jqhd", dscores, keys_w, preferred_element_type=jnp.float32
    ).reshape(rows, half)
    from_left = seq_shift(to_left.astype(jnp.bfloat16), 1)
    from_right = seq_shift(to_right.astype(jnp.bfloat16), -1)
    own = (
        total[halo : halo + rows]
        + jnp.pad(from_left.astype(jnp.float32), ((0, rows - halo), (0, 0)))
        + jnp.pad(from_right.astype(jnp.float32), ((rows - halo, 0), (0, 0)))
    )
    grad_k = own[:, :half].astype(jnp.bfloat16)
    grad_v = own[:, half:].astype(jnp.bfloat16)

    kv_pair = jnp.stack([grad_k, grad_v])
    qn_pair = jnp.stack([grad_q.astype(jnp.bfloat16), normed.astype(jnp.bfloat16)])
    keep_pair = jnp.where(is_first, kv_pair, qn_pair)
    back = sec_swap(jnp.where(is_first, qn_pair, kv_pair))
    result = jnp.where(
        is_first,
        jnp.concatenate([keep_pair, back], axis=2),
        jnp.concatenate([back, keep_pair], axis=2),
    )
    return result[None]


def solution(mesh):
    return jax.shard_map(
        per_device,
        mesh=mesh,
        in_specs=(P("sec", None, "seq", "mp"), P()),
        out_specs=P("sec", None, "seq", "mp"),
        check_vma=False,
    )
```

```python
import jax
import jax.numpy as jnp
from jax import lax
from jax.sharding import PartitionSpec as P

UNIT = 128
HEADS = 32
DH = 64
MAX_DOC_UNITS = 3


epsilon = 1e-06


def seq_shift(value, steps):
    count = lax.axis_size("seq")
    initial, last = (max(0, -steps), min(count, count - steps))
    return lax.ppermute(value, "seq", [(source, source + steps) for source in range(initial, last)])


def sec_swap(value):
    return lax.ppermute(value, "sec", [(0, 1), (1, 0)])


def window_plan(doc_units, seq_place, unit_count, halo_units):
    ends = jnp.cumsum(doc_units).astype(jnp.int32)
    first_unit = seq_place * unit_count
    query_units = first_unit + jnp.arange(unit_count, dtype=jnp.int32)

    def unit_doc(units):
        counted = jnp.sum((ends[None, :] <= units[:, None]).astype(jnp.int32), axis=1)
        return jnp.where(units < 0, jnp.int32(-1), counted)

    starts = jnp.max(
        jnp.where(ends[None, :] <= query_units[:, None], ends[None, :], 0), axis=1
    ).astype(jnp.int32)
    key_units = starts[:, None] + jnp.arange(MAX_DOC_UNITS, dtype=jnp.int32)[None, :]
    allowed = unit_doc(key_units.reshape(-1)).reshape(key_units.shape) == unit_doc(query_units)[:, None]
    return starts - (first_unit - halo_units), allowed


def attention_grads(queries, cotangent, pieces, rel_starts, allowed, total_fn, total_cols):
    rows, head_cols = queries.shape
    heads = head_cols // DH
    unit_count = rows // UNIT
    window = MAX_DOC_UNITS * UNIT
    score_scale = DH ** (-0.5)
    units = [piece[u * UNIT : (u + 1) * UNIT] for piece in pieces for u in range(piece.shape[0] // UNIT)]

    def candidate(first):
        return jnp.concatenate(units[first : first + MAX_DOC_UNITS], axis=0)

    joined_w = []
    for j in range(unit_count):
        offset = rel_starts[j] - j
        chosen = candidate(j + MAX_DOC_UNITS - 1)
        for shift in range(MAX_DOC_UNITS - 2, -1, -1):
            chosen = jnp.where(offset == shift, candidate(j + shift), chosen)
        joined_w.append(chosen)
    joined_w = jnp.stack(joined_w)
    keys_w = joined_w[:, :, :head_cols].reshape(unit_count, window, heads, DH)
    values_w = joined_w[:, :, head_cols:].reshape(unit_count, window, heads, DH)
    q4 = queries.reshape(unit_count, UNIT, heads, DH)
    cot_float = cotangent.astype(jnp.float32)

    mask = jnp.repeat(allowed, UNIT, axis=1)[:, None, None, :]
    scores = (
        jnp.einsum("jqhd,jkhd->jhqk", q4, keys_w, preferred_element_type=jnp.float32) * score_scale
    )
    scores = jnp.where(mask, scores, -jnp.inf)
    row_max = jnp.max(scores, axis=3, keepdims=True)
    expven = jnp.exp(scores - row_max)
    weights = expven / jnp.sum(expven, axis=3, keepdims=True)
    rounded = weights.astype(jnp.bfloat16)
    attended4 = jnp.einsum("jhqk,jkhd->jqhd", rounded, values_w, preferred_element_type=jnp.float32)
    attended = attended4.reshape(rows, head_cols)

    squares, crosses = total_fn(
        (jnp.sum(attended * attended, axis=1), jnp.sum(cot_float * attended, axis=1))
    )
    spread = jnp.sqrt(squares / total_cols + epsilon)
    normed = attended / spread[:, None]
    shared = crosses / total_cols / spread
    upstream = ((cot_float - normed * shared[:, None]) / spread[:, None]).astype(jnp.bfloat16)
    up4 = upstream.reshape(unit_count, UNIT, heads, DH)

    delta = jnp.sum(up4.astype(jnp.float32) * attended4, axis=3)
    delta = jnp.transpose(delta, (0, 2, 1))[..., None]
    dprobs = jnp.einsum("jqhd,jkhd->jhqk", up4, values_w, preferred_element_type=jnp.float32)
    dscores = (weights * (dprobs - delta) * score_scale).astype(jnp.bfloat16)
    grad_q = jnp.einsum("jhqk,jkhd->jqhd", dscores, keys_w, preferred_element_type=jnp.float32)
    grad_kw = jnp.einsum("jhqk,jqhd->jkhd", dscores, q4, preferred_element_type=jnp.float32)
    grad_vw = jnp.einsum("jhqk,jqhd->jkhd", rounded, up4, preferred_element_type=jnp.float32)
    grad_kvw = jnp.concatenate(
        [grad_kw.reshape(unit_count, window, head_cols), grad_vw.reshape(unit_count, window, head_cols)],
        axis=2,
    )
    near_rows = sum(piece.shape[0] for piece in pieces)
    total = jnp.zeros((near_rows, 2 * head_cols), jnp.float32)
    for j in range(unit_count):
        start = rel_starts[j] * UNIT
        total = lax.dynamic_update_slice_in_dim(
            total, lax.dynamic_slice_in_dim(total, start, window, 0) + grad_kvw[j], start, 0
        )
    return grad_q.reshape(rows, head_cols), normed, total


def per_device(heads_in, doc_units):
    section = lax.axis_index("sec")
    seq_place = lax.axis_index("seq")
    is_first = section == 0
    local_heads = heads_in[0]
    _, rows, cols = local_heads.shape
    half = cols // 2
    unit_count = rows // UNIT
    halo_units = MAX_DOC_UNITS - 1
    halo = halo_units * UNIT
    total_cols = cols * lax.axis_size("mp")

    keep_offset = section * half
    send_offset = (1 - section) * half
    sent = lax.dynamic_slice_in_dim(local_heads, send_offset, half, 2)
    kept = lax.dynamic_slice_in_dim(local_heads, keep_offset, half, 2)
    arrived = sec_swap(sent)
    key_value = jnp.where(is_first, kept, arrived)
    query_cot = jnp.where(is_first, arrived, kept)

    joined = jnp.concatenate([key_value[0], key_value[1]], axis=1)
    low = seq_shift(joined[rows - halo :], 1)
    high = seq_shift(joined[:halo], -1)

    rel_starts, allowed = window_plan(doc_units, seq_place, unit_count, halo_units)

    def row_total(sums_pair):
        sums = jnp.stack(sums_pair)
        sums = sums + sec_swap(sums)
        sums = sums + lax.ppermute(sums, "mp", [(0, 1), (1, 0)])
        return sums[0], sums[1]

    grad_q, normed, total = attention_grads(
        query_cot[0],
        query_cot[1],
        (low, joined, high),
        rel_starts,
        allowed,
        row_total,
        total_cols,
    )
    from_left = seq_shift(total[rows + halo :].astype(jnp.bfloat16), 1)
    from_right = seq_shift(total[:halo].astype(jnp.bfloat16), -1)
    own = (
        total[halo : halo + rows]
        + jnp.pad(from_left.astype(jnp.float32), ((0, rows - halo), (0, 0)))
        + jnp.pad(from_right.astype(jnp.float32), ((rows - halo, 0), (0, 0)))
    )
    grad_k = own[:, :half].astype(jnp.bfloat16)
    grad_v = own[:, half:].astype(jnp.bfloat16)

    kv_pair = jnp.stack([grad_k, grad_v])
    qn_pair = jnp.stack([grad_q.astype(jnp.bfloat16), normed.astype(jnp.bfloat16)])
    keep_pair = jnp.where(is_first, kv_pair, qn_pair)
    back = sec_swap(jnp.where(is_first, qn_pair, kv_pair))
    result = jnp.where(
        is_first,
        jnp.concatenate([keep_pair, back], axis=2),
        jnp.concatenate([back, keep_pair], axis=2),
    )
    return result[None]


def solution(mesh):
    return jax.shard_map(
        per_device,
        mesh=mesh,
        in_specs=(P("sec", None, "seq", "mp"), P()),
        out_specs=P("sec", None, "seq", "mp"),
        check_vma=False,
    )
```

```python
import jax
import jax.numpy as jnp
from jax import lax
from jax.sharding import PartitionSpec as P

UNIT = 128
HEADS = 32
DH = 64
MAX_DOC_UNITS = 3


epsilon = 1e-06


def seq_shift(value, steps):
    count = lax.axis_size("seq")
    initial, last = (max(0, -steps), min(count, count - steps))
    return lax.ppermute(value, "seq", [(source, source + steps) for source in range(initial, last)])


def sec_swap(value):
    return lax.ppermute(value, "sec", [(0, 1), (1, 0)])


def window_plan(doc_units, seq_place, unit_count, halo_units):
    ends = jnp.cumsum(doc_units).astype(jnp.int32)
    first_unit = seq_place * unit_count
    query_units = first_unit + jnp.arange(unit_count, dtype=jnp.int32)

    def unit_doc(units):
        counted = jnp.sum((ends[None, :] <= units[:, None]).astype(jnp.int32), axis=1)
        return jnp.where(units < 0, jnp.int32(-1), counted)

    starts = jnp.max(
        jnp.where(ends[None, :] <= query_units[:, None], ends[None, :], 0), axis=1
    ).astype(jnp.int32)
    key_units = starts[:, None] + jnp.arange(MAX_DOC_UNITS, dtype=jnp.int32)[None, :]
    allowed = unit_doc(key_units.reshape(-1)).reshape(key_units.shape) == unit_doc(query_units)[:, None]
    return starts - (first_unit - halo_units), allowed


def attention_grads(queries, cotangent, near_keys, near_values, rel_starts, allowed, total_fn, total_cols):
    rows, head_cols = queries.shape
    heads = head_cols // DH
    unit_count = rows // UNIT
    window = MAX_DOC_UNITS * UNIT
    score_scale = DH ** (-0.5)

    def windows(near):
        pieces = [
            lax.dynamic_slice_in_dim(near, rel_starts[j] * UNIT, window, 0) for j in range(unit_count)
        ]
        return jnp.stack(pieces).reshape(unit_count, window, heads, DH)

    keys_w = windows(near_keys)
    values_w = windows(near_values)
    q4 = queries.reshape(unit_count, UNIT, heads, DH)
    cot_float = cotangent.astype(jnp.float32)

    mask = jnp.repeat(allowed, UNIT, axis=1)[:, None, None, :]
    scores = (
        jnp.einsum("jqhd,jkhd->jhqk", q4, keys_w, preferred_element_type=jnp.float32) * score_scale
    )
    scores = jnp.where(mask, scores, -jnp.inf)
    row_max = jnp.max(scores, axis=3, keepdims=True)
    expven = jnp.exp(scores - row_max)
    weights = expven * (1.0 / jnp.sum(expven, axis=3, keepdims=True))
    rounded = weights.astype(jnp.bfloat16)
    attended4 = jnp.einsum("jhqk,jkhd->jqhd", rounded, values_w, preferred_element_type=jnp.float32)
    attended = attended4.reshape(rows, head_cols)

    squares, crosses = total_fn(
        (jnp.sum(attended * attended, axis=1), jnp.sum(cot_float * attended, axis=1))
    )
    spread = jnp.sqrt(squares / total_cols + epsilon)
    inverse = 1.0 / spread
    normed = attended * inverse[:, None]
    shared = crosses / total_cols * inverse
    upstream = ((cot_float - normed * shared[:, None]) * inverse[:, None]).astype(jnp.bfloat16)
    up4 = upstream.reshape(unit_count, UNIT, heads, DH)

    delta = jnp.sum(up4.astype(jnp.float32) * attended4, axis=3)
    delta = jnp.transpose(delta, (0, 2, 1))[..., None]
    dprobs = jnp.einsum("jqhd,jkhd->jhqk", up4, values_w, preferred_element_type=jnp.float32)
    dscores = (weights * (dprobs - delta) * score_scale).astype(jnp.bfloat16)
    grad_q = jnp.einsum("jhqk,jkhd->jqhd", dscores, keys_w, preferred_element_type=jnp.float32)
    grad_kw = jnp.einsum("jhqk,jqhd->jkhd", dscores, q4, preferred_element_type=jnp.float32)
    grad_vw = jnp.einsum("jhqk,jqhd->jkhd", rounded, up4, preferred_element_type=jnp.float32)
    grad_kvw = jnp.concatenate(
        [grad_kw.reshape(unit_count, window, head_cols), grad_vw.reshape(unit_count, window, head_cols)],
        axis=2,
    )
    near_rows = near_keys.shape[0]
    total = jnp.zeros((near_rows, 2 * head_cols), jnp.float32)
    for j in range(unit_count):
        start = rel_starts[j] * UNIT
        total = lax.dynamic_update_slice_in_dim(
            total, lax.dynamic_slice_in_dim(total, start, window, 0) + grad_kvw[j], start, 0
        )
    return grad_q.reshape(rows, head_cols), normed, total


def per_device(heads_in, doc_units):
    section = lax.axis_index("sec")
    seq_place = lax.axis_index("seq")
    is_first = section == 0
    local_heads = heads_in[0]
    _, rows, cols = local_heads.shape
    half = cols // 2
    unit_count = rows // UNIT
    halo_units = MAX_DOC_UNITS - 1
    halo = halo_units * UNIT
    total_cols = cols * lax.axis_size("mp")

    keep_offset = section * half
    send_offset = (1 - section) * half
    sent = lax.dynamic_slice_in_dim(local_heads, send_offset, half, 2)
    kept = lax.dynamic_slice_in_dim(local_heads, keep_offset, half, 2)
    arrived = sec_swap(sent)
    key_value = jnp.where(is_first, kept, arrived)
    query_cot = jnp.where(is_first, arrived, kept)

    joined = jnp.concatenate([key_value[0], key_value[1]], axis=1)
    low = seq_shift(joined[rows - halo :], 1)
    high = seq_shift(joined[:halo], -1)
    near = jnp.concatenate([low, joined, high], axis=0)

    rel_starts, allowed = window_plan(doc_units, seq_place, unit_count, halo_units)

    def row_total(sums_pair):
        sums = jnp.stack(sums_pair)
        sums = sums + sec_swap(sums)
        sums = sums + lax.ppermute(sums, "mp", [(0, 1), (1, 0)])
        return sums[0], sums[1]

    grad_q, normed, total = attention_grads(
        query_cot[0],
        query_cot[1],
        near[:, :half],
        near[:, half:],
        rel_starts,
        allowed,
        row_total,
        total_cols,
    )
    from_left = seq_shift(total[near.shape[0] - halo :].astype(jnp.bfloat16), 1)
    from_right = seq_shift(total[:halo].astype(jnp.bfloat16), -1)
    own = (
        total[halo : halo + rows]
        + jnp.pad(from_left.astype(jnp.float32), ((0, rows - halo), (0, 0)))
        + jnp.pad(from_right.astype(jnp.float32), ((rows - halo, 0), (0, 0)))
    )
    grad_k = own[:, :half].astype(jnp.bfloat16)
    grad_v = own[:, half:].astype(jnp.bfloat16)

    kv_pair = jnp.stack([grad_k, grad_v])
    qn_pair = jnp.stack([grad_q.astype(jnp.bfloat16), normed.astype(jnp.bfloat16)])
    keep_pair = jnp.where(is_first, kv_pair, qn_pair)
    back = sec_swap(jnp.where(is_first, qn_pair, kv_pair))
    result = jnp.where(
        is_first,
        jnp.concatenate([keep_pair, back], axis=2),
        jnp.concatenate([back, keep_pair], axis=2),
    )
    return result[None]


def solution(mesh):
    return jax.shard_map(
        per_device,
        mesh=mesh,
        in_specs=(P("sec", None, "seq", "mp"), P()),
        out_specs=P("sec", None, "seq", "mp"),
        check_vma=False,
    )
```

```python
import jax
import jax.numpy as jnp
from jax import lax
from jax.sharding import PartitionSpec as P

UNIT = 128
HEADS = 32
DH = 64
MAX_DOC_UNITS = 3


epsilon = 1e-06


def seq_shift(value, steps):
    count = lax.axis_size("seq")
    initial, last = (max(0, -steps), min(count, count - steps))
    return lax.ppermute(value, "seq", [(source, source + steps) for source in range(initial, last)])


def sec_swap(value):
    return lax.ppermute(value, "sec", [(0, 1), (1, 0)])


def window_plan(doc_units, seq_place, unit_count, halo_units):
    ends = jnp.cumsum(doc_units).astype(jnp.int32)
    first_unit = seq_place * unit_count
    query_units = first_unit + jnp.arange(unit_count, dtype=jnp.int32)

    def unit_doc(units):
        counted = jnp.sum((ends[None, :] <= units[:, None]).astype(jnp.int32), axis=1)
        return jnp.where(units < 0, jnp.int32(-1), counted)

    starts = jnp.max(
        jnp.where(ends[None, :] <= query_units[:, None], ends[None, :], 0), axis=1
    ).astype(jnp.int32)
    key_units = starts[:, None] + jnp.arange(MAX_DOC_UNITS, dtype=jnp.int32)[None, :]
    allowed = unit_doc(key_units.reshape(-1)).reshape(key_units.shape) == unit_doc(query_units)[:, None]
    return starts - (first_unit - halo_units), allowed


def attention_grads(queries, cotangent, near_keys, near_values, rel_starts, allowed, total_fn, total_cols):
    rows, head_cols = queries.shape
    heads = head_cols // DH
    unit_count = rows // UNIT
    window = MAX_DOC_UNITS * UNIT
    score_scale = DH ** (-0.5)

    def windows(near):
        pieces = [
            lax.dynamic_slice_in_dim(near, rel_starts[j] * UNIT, window, 0) for j in range(unit_count)
        ]
        return jnp.stack(pieces).reshape(unit_count, window, heads, DH)

    keys_w = windows(near_keys)
    values_w = windows(near_values)
    q4 = queries.reshape(unit_count, UNIT, heads, DH)
    cot_float = cotangent.astype(jnp.float32)

    mask = jnp.repeat(allowed, UNIT, axis=1)[:, None, None, :]
    scores = (
        jnp.einsum("jqhd,jkhd->jhqk", q4, keys_w, preferred_element_type=jnp.float32) * score_scale
    )
    scores = jnp.where(mask, scores, -jnp.inf)
    row_max = jnp.max(scores, axis=3, keepdims=True)
    expven = jnp.exp(scores - row_max)
    weights = expven / jnp.sum(expven, axis=3, keepdims=True)
    rounded = weights.astype(jnp.bfloat16)
    attended4 = jnp.einsum("jhqk,jkhd->jqhd", rounded, values_w, preferred_element_type=jnp.float32)
    attended = attended4.reshape(rows, head_cols)

    squares, crosses = total_fn(
        (jnp.sum(attended * attended, axis=1), jnp.sum(cot_float * attended, axis=1))
    )
    spread = jnp.sqrt(squares / total_cols + epsilon)
    normed = attended / spread[:, None]
    shared = crosses / total_cols / spread
    upstream = ((cot_float - normed * shared[:, None]) / spread[:, None]).astype(jnp.bfloat16)
    up4 = upstream.reshape(unit_count, UNIT, heads, DH)

    delta = jnp.sum(up4.astype(jnp.float32) * attended4, axis=3)
    delta = jnp.transpose(delta, (0, 2, 1))[..., None]
    dprobs = jnp.einsum("jqhd,jkhd->jhqk", up4, values_w, preferred_element_type=jnp.float32)
    dscores = (weights * (dprobs - delta) * score_scale).astype(jnp.bfloat16)
    grad_q = jnp.einsum("jhqk,jkhd->jqhd", dscores, keys_w, preferred_element_type=jnp.float32)
    grad_kw = jnp.einsum("jhqk,jqhd->jkhd", dscores, q4, preferred_element_type=jnp.float32)
    grad_vw = jnp.einsum("jhqk,jqhd->jkhd", rounded, up4, preferred_element_type=jnp.float32)
    grad_kvw = jnp.concatenate(
        [grad_kw.reshape(unit_count, window, head_cols), grad_vw.reshape(unit_count, window, head_cols)],
        axis=2,
    )
    near_rows = near_keys.shape[0]
    total = jnp.zeros((near_rows, 2 * head_cols), jnp.float32)
    for j in range(unit_count):
        start = rel_starts[j] * UNIT
        total = lax.dynamic_update_slice_in_dim(
            total, lax.dynamic_slice_in_dim(total, start, window, 0) + grad_kvw[j], start, 0
        )
    return grad_q.reshape(rows, head_cols), normed, total


def per_device(heads_in, doc_units):
    section = lax.axis_index("sec")
    seq_place = lax.axis_index("seq")
    is_first = section == 0
    local_heads = heads_in[0]
    _, rows, cols = local_heads.shape
    half = cols // 2
    unit_count = rows // UNIT
    halo_units = MAX_DOC_UNITS - 1
    halo = halo_units * UNIT
    total_cols = cols * lax.axis_size("mp")

    keep_offset = section * half
    send_offset = (1 - section) * half
    sent = lax.dynamic_slice_in_dim(local_heads, send_offset, half, 2)
    arrived = sec_swap(sent)
    arrived, later_heads = lax.optimization_barrier((arrived, local_heads))
    kept = lax.dynamic_slice_in_dim(later_heads, keep_offset, half, 2)
    key_value = jnp.where(is_first, kept, arrived)
    query_cot = jnp.where(is_first, arrived, kept)

    joined = jnp.concatenate([key_value[0], key_value[1]], axis=1)
    low = seq_shift(joined[rows - halo :], 1)
    high = seq_shift(joined[:halo], -1)
    near = jnp.concatenate([low, joined, high], axis=0)

    rel_starts, allowed = window_plan(doc_units, seq_place, unit_count, halo_units)

    def row_total(sums_pair):
        sums = jnp.stack(sums_pair)
        sums = sums + sec_swap(sums)
        sums = sums + lax.ppermute(sums, "mp", [(0, 1), (1, 0)])
        return sums[0], sums[1]

    grad_q, normed, total = attention_grads(
        query_cot[0],
        query_cot[1],
        near[:, :half],
        near[:, half:],
        rel_starts,
        allowed,
        row_total,
        total_cols,
    )
    from_left = seq_shift(total[near.shape[0] - halo :].astype(jnp.bfloat16), 1)
    from_right = seq_shift(total[:halo].astype(jnp.bfloat16), -1)
    own = (
        total[halo : halo + rows]
        + jnp.pad(from_left.astype(jnp.float32), ((0, rows - halo), (0, 0)))
        + jnp.pad(from_right.astype(jnp.float32), ((rows - halo, 0), (0, 0)))
    )
    grad_k = own[:, :half].astype(jnp.bfloat16)
    grad_v = own[:, half:].astype(jnp.bfloat16)

    kv_pair = jnp.stack([grad_k, grad_v])
    qn_pair = jnp.stack([grad_q.astype(jnp.bfloat16), normed.astype(jnp.bfloat16)])
    keep_pair = jnp.where(is_first, kv_pair, qn_pair)
    back = sec_swap(jnp.where(is_first, qn_pair, kv_pair))
    result = jnp.where(
        is_first,
        jnp.concatenate([keep_pair, back], axis=2),
        jnp.concatenate([back, keep_pair], axis=2),
    )
    return result[None]


def solution(mesh):
    return jax.shard_map(
        per_device,
        mesh=mesh,
        in_specs=(P("sec", None, "seq", "mp"), P()),
        out_specs=P("sec", None, "seq", "mp"),
        check_vma=False,
    )
```

```python
import jax
import jax.numpy as jnp
from jax import lax
from jax.sharding import PartitionSpec as P

UNIT = 128
HEADS = 32
DH = 64
MAX_DOC_UNITS = 3


epsilon = 1e-06


def seq_shift(value, steps):
    count = lax.axis_size("seq")
    initial, last = (max(0, -steps), min(count, count - steps))
    return lax.ppermute(value, "seq", [(source, source + steps) for source in range(initial, last)])


def sec_swap(value):
    return lax.ppermute(value, "sec", [(0, 1), (1, 0)])


def window_plan(doc_units, seq_place, unit_count, halo_units):
    ends = jnp.cumsum(doc_units).astype(jnp.int32)
    first_unit = seq_place * unit_count
    query_units = first_unit + jnp.arange(unit_count, dtype=jnp.int32)

    def unit_doc(units):
        counted = jnp.sum((ends[None, :] <= units[:, None]).astype(jnp.int32), axis=1)
        return jnp.where(units < 0, jnp.int32(-1), counted)

    starts = jnp.max(
        jnp.where(ends[None, :] <= query_units[:, None], ends[None, :], 0), axis=1
    ).astype(jnp.int32)
    key_units = starts[:, None] + jnp.arange(MAX_DOC_UNITS, dtype=jnp.int32)[None, :]
    allowed = unit_doc(key_units.reshape(-1)).reshape(key_units.shape) == unit_doc(query_units)[:, None]
    return starts - (first_unit - halo_units), allowed


def attention_grads(queries, cotangent, near_keys, near_values, rel_starts, allowed, total_fn, total_cols):
    rows, head_cols = queries.shape
    heads = head_cols // DH
    unit_count = rows // UNIT
    window = MAX_DOC_UNITS * UNIT
    score_scale = DH ** (-0.5)

    def windows(near):
        pieces = [
            lax.dynamic_slice_in_dim(near, rel_starts[j] * UNIT, window, 0) for j in range(unit_count)
        ]
        return jnp.stack(pieces).reshape(unit_count, window, heads, DH)

    keys_w = windows(near_keys)
    values_w = windows(near_values)
    q4 = queries.reshape(unit_count, UNIT, heads, DH)
    cot_float = cotangent.astype(jnp.float32)

    mask = jnp.repeat(allowed, UNIT, axis=1)[:, None, None, :]
    scores = (
        jnp.einsum("jqhd,jkhd->jhqk", q4, keys_w, preferred_element_type=jnp.float32) * score_scale
    )
    scores = jnp.where(mask, scores, -jnp.inf)
    row_max = jnp.max(scores, axis=3, keepdims=True)
    expven = jnp.exp(scores - row_max)
    weights = expven / jnp.sum(expven, axis=3, keepdims=True)
    rounded = weights.astype(jnp.bfloat16)
    attended4 = jnp.einsum("jhqk,jkhd->jqhd", rounded, values_w, preferred_element_type=jnp.float32)
    attended = attended4.reshape(rows, head_cols)

    squares, crosses = total_fn(
        (jnp.sum(attended * attended, axis=1), jnp.sum(cot_float * attended, axis=1))
    )
    spread = jnp.sqrt(squares / total_cols + epsilon)
    normed = attended / spread[:, None]
    shared = crosses / total_cols / spread
    upstream = ((cot_float - normed * shared[:, None]) / spread[:, None]).astype(jnp.bfloat16)
    up4 = upstream.reshape(unit_count, UNIT, heads, DH)

    delta = jnp.sum(up4.astype(jnp.float32) * attended4, axis=3)
    delta = jnp.transpose(delta, (0, 2, 1))[..., None]
    dprobs = jnp.einsum("jqhd,jkhd->jhqk", up4, values_w, preferred_element_type=jnp.float32)
    dscores = (weights * (dprobs - delta) * score_scale).astype(jnp.bfloat16)
    grad_q = jnp.einsum("jhqk,jkhd->jqhd", dscores, keys_w, preferred_element_type=jnp.float32)
    grad_kw = jnp.einsum("jhqk,jqhd->jkhd", dscores, q4, preferred_element_type=jnp.float32)
    grad_vw = jnp.einsum("jhqk,jqhd->jkhd", rounded, up4, preferred_element_type=jnp.float32)
    grad_kvw = jnp.concatenate(
        [grad_kw.reshape(unit_count, window, head_cols), grad_vw.reshape(unit_count, window, head_cols)],
        axis=2,
    )
    near_rows = near_keys.shape[0]
    total = jnp.zeros((near_rows, 2 * head_cols), jnp.float32)
    for j in range(unit_count):
        start = rel_starts[j] * UNIT
        total = lax.dynamic_update_slice_in_dim(
            total, lax.dynamic_slice_in_dim(total, start, window, 0) + grad_kvw[j], start, 0
        )
    return grad_q.reshape(rows, head_cols), normed, total


def per_device(heads_in, doc_units):
    section = lax.axis_index("sec")
    seq_place = lax.axis_index("seq")
    is_first = section == 0
    local_heads = heads_in[0]
    _, rows, cols = local_heads.shape
    heads = cols // DH
    heads_first = -(-heads * 3 // 5)
    width = heads_first * DH
    width_second = cols - width
    unit_count = rows // UNIT
    halo_units = MAX_DOC_UNITS - 1
    halo = halo_units * UNIT
    total_cols = cols * lax.axis_size("mp")

    to_first = local_heads[:, :, :width]
    to_second = local_heads[:, :, width:]
    got_first = lax.ppermute(to_first, "sec", [(1, 0)])
    got_second = lax.ppermute(to_second, "sec", [(0, 1)])
    pad = jnp.zeros((2, rows, width - width_second), local_heads.dtype)
    key_value = jnp.where(is_first, to_first, jnp.concatenate([got_second, pad], axis=2))
    query_cot = jnp.where(is_first, got_first, jnp.concatenate([to_second, pad], axis=2))

    joined = jnp.concatenate([key_value[0], key_value[1]], axis=1)
    low = seq_shift(joined[rows - halo :], 1)
    high = seq_shift(joined[:halo], -1)
    near = jnp.concatenate([low, joined, high], axis=0)

    rel_starts, allowed = window_plan(doc_units, seq_place, unit_count, halo_units)

    def row_total(sums_pair):
        sums = jnp.stack(sums_pair)
        sums = sums + sec_swap(sums)
        sums = sums + lax.ppermute(sums, "mp", [(0, 1), (1, 0)])
        return sums[0], sums[1]

    grad_q, normed, total = attention_grads(
        query_cot[0],
        query_cot[1],
        near[:, :width],
        near[:, width:],
        rel_starts,
        allowed,
        row_total,
        total_cols,
    )
    normed = normed.astype(jnp.bfloat16)
    normed_first = lax.ppermute(normed, "sec", [(0, 1)])
    from_left = seq_shift(total[near.shape[0] - halo :].astype(jnp.bfloat16), 1)
    from_right = seq_shift(total[:halo].astype(jnp.bfloat16), -1)
    own = (
        total[halo : halo + rows]
        + jnp.pad(from_left.astype(jnp.float32), ((0, rows - halo), (0, 0)))
        + jnp.pad(from_right.astype(jnp.float32), ((rows - halo, 0), (0, 0)))
    )
    grad_k = own[:, :width].astype(jnp.bfloat16)
    grad_v = own[:, width:].astype(jnp.bfloat16)
    grad_q = grad_q.astype(jnp.bfloat16)

    common = max(width, 2 * width_second)

    def widened(value):
        return jnp.pad(value, ((0, 0), (0, common - value.shape[1])))

    second_out = jnp.concatenate([grad_k[:, :width_second], grad_v[:, :width_second]], axis=1)
    back = sec_swap(jnp.where(is_first, widened(grad_q), widened(second_out)))
    first_result = jnp.stack(
        [
            jnp.concatenate([grad_k, back[:, :width_second]], axis=1),
            jnp.concatenate([grad_v, back[:, width_second : 2 * width_second]], axis=1),
        ]
    )
    second_result = jnp.stack(
        [
            jnp.concatenate([back[:, :width], grad_q[:, :width_second]], axis=1),
            jnp.concatenate([normed_first, normed[:, :width_second]], axis=1),
        ]
    )
    return jnp.where(is_first, first_result, second_result)[None]


def solution(mesh):
    return jax.shard_map(
        per_device,
        mesh=mesh,
        in_specs=(P("sec", None, "seq", "mp"), P()),
        out_specs=P("sec", None, "seq", "mp"),
        check_vma=False,
    )
```

```python
import jax
import jax.numpy as jnp
from jax import lax
from jax.sharding import PartitionSpec as P

UNIT = 128
HEADS = 32
DH = 64
MAX_DOC_UNITS = 3


epsilon = 1e-06


def seq_shift(value, steps):
    count = lax.axis_size("seq")
    initial, last = (max(0, -steps), min(count, count - steps))
    return lax.ppermute(value, "seq", [(source, source + steps) for source in range(initial, last)])


def halo_swap(top, bottom):
    count = lax.axis_size("seq")
    even = lax.axis_index("seq") % 2 == 0
    inside = [(i, i ^ 1) for i in range(count) if (i ^ 1) < count]
    between = [(i, i + 1) for i in range(1, count - 1, 2)] + [(i + 1, i) for i in range(1, count - 1, 2)]
    within = lax.ppermute(jnp.where(even, bottom, top), "seq", inside)
    across = lax.ppermute(jnp.where(even, top, bottom), "seq", between)
    from_below = jnp.where(even, across, within)
    from_above = jnp.where(even, within, across)
    return from_below, from_above


def sec_swap(value):
    return lax.ppermute(value, "sec", [(0, 1), (1, 0)])


def window_plan(doc_units, seq_place, unit_count, halo_units):
    ends = jnp.cumsum(doc_units).astype(jnp.int32)
    first_unit = seq_place * unit_count
    query_units = first_unit + jnp.arange(unit_count, dtype=jnp.int32)

    def unit_doc(units):
        counted = jnp.sum((ends[None, :] <= units[:, None]).astype(jnp.int32), axis=1)
        return jnp.where(units < 0, jnp.int32(-1), counted)

    starts = jnp.max(
        jnp.where(ends[None, :] <= query_units[:, None], ends[None, :], 0), axis=1
    ).astype(jnp.int32)
    key_units = starts[:, None] + jnp.arange(MAX_DOC_UNITS, dtype=jnp.int32)[None, :]
    allowed = unit_doc(key_units.reshape(-1)).reshape(key_units.shape) == unit_doc(query_units)[:, None]
    return starts - (first_unit - halo_units), allowed


def attention_grads(queries, cotangent, near_keys, near_values, rel_starts, allowed, total_fn, total_cols):
    rows, head_cols = queries.shape
    heads = head_cols // DH
    unit_count = rows // UNIT
    window = MAX_DOC_UNITS * UNIT
    score_scale = DH ** (-0.5)

    def windows(near):
        pieces = [
            lax.dynamic_slice_in_dim(near, rel_starts[j] * UNIT, window, 0) for j in range(unit_count)
        ]
        return jnp.stack(pieces).reshape(unit_count, window, heads, DH)

    keys_w = windows(near_keys)
    values_w = windows(near_values)
    q4 = queries.reshape(unit_count, UNIT, heads, DH)
    cot_float = cotangent.astype(jnp.float32)

    mask = jnp.repeat(allowed, UNIT, axis=1)[:, None, None, :]
    scores = (
        jnp.einsum("jqhd,jkhd->jhqk", q4, keys_w, preferred_element_type=jnp.float32) * score_scale
    )
    scores = jnp.where(mask, scores, -jnp.inf)
    row_max = jnp.max(scores, axis=3, keepdims=True)
    expven = jnp.exp(scores - row_max)
    weights = expven / jnp.sum(expven, axis=3, keepdims=True)
    rounded = weights.astype(jnp.bfloat16)
    attended4 = jnp.einsum("jhqk,jkhd->jqhd", rounded, values_w, preferred_element_type=jnp.float32)
    attended = attended4.reshape(rows, head_cols)

    squares, crosses = total_fn(
        (jnp.sum(attended * attended, axis=1), jnp.sum(cot_float * attended, axis=1))
    )
    spread = jnp.sqrt(squares / total_cols + epsilon)
    normed = attended / spread[:, None]
    shared = crosses / total_cols / spread
    upstream = ((cot_float - normed * shared[:, None]) / spread[:, None]).astype(jnp.bfloat16)
    up4 = upstream.reshape(unit_count, UNIT, heads, DH)

    delta = jnp.sum(up4.astype(jnp.float32) * attended4, axis=3)
    delta = jnp.transpose(delta, (0, 2, 1))[..., None]
    dprobs = jnp.einsum("jqhd,jkhd->jhqk", up4, values_w, preferred_element_type=jnp.float32)
    dscores = (weights * (dprobs - delta) * score_scale).astype(jnp.bfloat16)
    grad_q = jnp.einsum("jhqk,jkhd->jqhd", dscores, keys_w, preferred_element_type=jnp.float32)
    grad_kw = jnp.einsum("jhqk,jqhd->jkhd", dscores, q4, preferred_element_type=jnp.float32)
    grad_vw = jnp.einsum("jhqk,jqhd->jkhd", rounded, up4, preferred_element_type=jnp.float32)
    grad_kvw = jnp.concatenate(
        [grad_kw.reshape(unit_count, window, head_cols), grad_vw.reshape(unit_count, window, head_cols)],
        axis=2,
    )
    near_rows = near_keys.shape[0]
    total = jnp.zeros((near_rows, 2 * head_cols), jnp.float32)
    for j in range(unit_count):
        start = rel_starts[j] * UNIT
        total = lax.dynamic_update_slice_in_dim(
            total, lax.dynamic_slice_in_dim(total, start, window, 0) + grad_kvw[j], start, 0
        )
    return grad_q.reshape(rows, head_cols), normed, total


def per_device(heads_in, doc_units):
    section = lax.axis_index("sec")
    seq_place = lax.axis_index("seq")
    is_first = section == 0
    local_heads = heads_in[0]
    _, rows, cols = local_heads.shape
    half = cols // 2
    unit_count = rows // UNIT
    halo_units = MAX_DOC_UNITS - 1
    halo = halo_units * UNIT
    total_cols = cols * lax.axis_size("mp")

    keep_offset = section * half
    send_offset = (1 - section) * half
    sent = lax.dynamic_slice_in_dim(local_heads, send_offset, half, 2)
    kept = lax.dynamic_slice_in_dim(local_heads, keep_offset, half, 2)
    arrived = sec_swap(sent)
    key_value = jnp.where(is_first, kept, arrived)
    query_cot = jnp.where(is_first, arrived, kept)

    joined = jnp.concatenate([key_value[0], key_value[1]], axis=1)
    low, high = halo_swap(joined[:halo], joined[rows - halo :])
    near = jnp.concatenate([low, joined, high], axis=0)

    rel_starts, allowed = window_plan(doc_units, seq_place, unit_count, halo_units)

    def row_total(sums_pair):
        sums = jnp.stack(sums_pair)
        sums = sums + sec_swap(sums)
        sums = sums + lax.ppermute(sums, "mp", [(0, 1), (1, 0)])
        return sums[0], sums[1]

    grad_q, normed, total = attention_grads(
        query_cot[0],
        query_cot[1],
        near[:, :half],
        near[:, half:],
        rel_starts,
        allowed,
        row_total,
        total_cols,
    )
    from_left, from_right = halo_swap(
        total[:halo].astype(jnp.bfloat16), total[near.shape[0] - halo :].astype(jnp.bfloat16)
    )
    own = (
        total[halo : halo + rows]
        + jnp.pad(from_left.astype(jnp.float32), ((0, rows - halo), (0, 0)))
        + jnp.pad(from_right.astype(jnp.float32), ((rows - halo, 0), (0, 0)))
    )
    grad_k = own[:, :half].astype(jnp.bfloat16)
    grad_v = own[:, half:].astype(jnp.bfloat16)

    kv_pair = jnp.stack([grad_k, grad_v])
    qn_pair = jnp.stack([grad_q.astype(jnp.bfloat16), normed.astype(jnp.bfloat16)])
    keep_pair = jnp.where(is_first, kv_pair, qn_pair)
    back = sec_swap(jnp.where(is_first, qn_pair, kv_pair))
    result = jnp.where(
        is_first,
        jnp.concatenate([keep_pair, back], axis=2),
        jnp.concatenate([back, keep_pair], axis=2),
    )
    return result[None]


def solution(mesh):
    return jax.shard_map(
        per_device,
        mesh=mesh,
        in_specs=(P("sec", None, "seq", "mp"), P()),
        out_specs=P("sec", None, "seq", "mp"),
        check_vma=False,
    )
```

```python
import jax
import jax.numpy as jnp
from jax import lax
from jax.sharding import PartitionSpec as P

UNIT = 128
HEADS = 32
DH = 64
MAX_DOC_UNITS = 3


epsilon = 1e-06


def seq_shift(value, steps):
    count = lax.axis_size("seq")
    initial, last = (max(0, -steps), min(count, count - steps))
    return lax.ppermute(value, "seq", [(source, source + steps) for source in range(initial, last)])


def halo_swap(top, bottom):
    count = lax.axis_size("seq")
    even = lax.axis_index("seq") % 2 == 0
    inside = [(i, i ^ 1) for i in range(count) if (i ^ 1) < count]
    between = [(i, i + 1) for i in range(1, count - 1, 2)] + [(i + 1, i) for i in range(1, count - 1, 2)]
    within = lax.ppermute(jnp.where(even, bottom, top), "seq", inside)
    across = lax.ppermute(jnp.where(even, top, bottom), "seq", between)
    from_below = jnp.where(even, across, within)
    from_above = jnp.where(even, within, across)
    return from_below, from_above


def sec_swap(value):
    return lax.ppermute(value, "sec", [(0, 1), (1, 0)])


def window_plan(doc_units, seq_place, unit_count, halo_units):
    ends = jnp.cumsum(doc_units).astype(jnp.int32)
    first_unit = seq_place * unit_count
    query_units = first_unit + jnp.arange(unit_count, dtype=jnp.int32)

    def unit_doc(units):
        counted = jnp.sum((ends[None, :] <= units[:, None]).astype(jnp.int32), axis=1)
        return jnp.where(units < 0, jnp.int32(-1), counted)

    starts = jnp.max(
        jnp.where(ends[None, :] <= query_units[:, None], ends[None, :], 0), axis=1
    ).astype(jnp.int32)
    key_units = starts[:, None] + jnp.arange(MAX_DOC_UNITS, dtype=jnp.int32)[None, :]
    allowed = unit_doc(key_units.reshape(-1)).reshape(key_units.shape) == unit_doc(query_units)[:, None]
    return starts - (first_unit - halo_units), allowed


def attention_grads(queries, cotangent, near_keys, near_values, rel_starts, allowed, total_fn, total_cols):
    rows, head_cols = queries.shape
    heads = head_cols // DH
    unit_count = rows // UNIT
    window = MAX_DOC_UNITS * UNIT
    score_scale = DH ** (-0.5)

    def windows(near):
        pieces = [
            lax.dynamic_slice_in_dim(near, rel_starts[j] * UNIT, window, 0) for j in range(unit_count)
        ]
        return jnp.stack(pieces).reshape(unit_count, window, heads, DH)

    keys_w = windows(near_keys)
    values_w = windows(near_values)
    q4 = queries.reshape(unit_count, UNIT, heads, DH)
    cot_float = cotangent.astype(jnp.float32)

    mask = jnp.repeat(allowed, UNIT, axis=1)[:, None, None, :]
    scores = (
        jnp.einsum("jqhd,jkhd->jhqk", q4, keys_w, preferred_element_type=jnp.float32) * score_scale
    )
    scores = jnp.where(mask, scores, -jnp.inf)
    row_max = jnp.max(scores, axis=3, keepdims=True)
    expven = jnp.exp(scores - row_max)
    weights = expven / jnp.sum(expven, axis=3, keepdims=True)
    rounded = weights.astype(jnp.bfloat16)
    attended4 = jnp.einsum("jhqk,jkhd->jqhd", rounded, values_w, preferred_element_type=jnp.float32)
    attended = attended4.reshape(rows, head_cols)

    squares, crosses = total_fn(
        (jnp.sum(attended * attended, axis=1), jnp.sum(cot_float * attended, axis=1))
    )
    spread = jnp.sqrt(squares / total_cols + epsilon)
    normed = attended / spread[:, None]
    shared = crosses / total_cols / spread
    upstream = ((cot_float - normed * shared[:, None]) / spread[:, None]).astype(jnp.bfloat16)
    up4 = upstream.reshape(unit_count, UNIT, heads, DH)

    delta = jnp.sum(up4.astype(jnp.float32) * attended4, axis=3)
    delta = jnp.transpose(delta, (0, 2, 1))[..., None]
    dprobs = jnp.einsum("jqhd,jkhd->jhqk", up4, values_w, preferred_element_type=jnp.float32)
    dscores = (weights * (dprobs - delta) * score_scale).astype(jnp.bfloat16)
    grad_q = jnp.einsum("jhqk,jkhd->jqhd", dscores, keys_w, preferred_element_type=jnp.float32)
    grad_kw = jnp.einsum("jhqk,jqhd->jkhd", dscores, q4, preferred_element_type=jnp.float32)
    grad_vw = jnp.einsum("jhqk,jqhd->jkhd", rounded, up4, preferred_element_type=jnp.float32)
    grad_kvw = jnp.concatenate(
        [grad_kw.reshape(unit_count, window, head_cols), grad_vw.reshape(unit_count, window, head_cols)],
        axis=2,
    )
    near_rows = near_keys.shape[0]
    total = jnp.zeros((near_rows, 2 * head_cols), jnp.float32)
    for j in range(unit_count):
        start = rel_starts[j] * UNIT
        total = lax.dynamic_update_slice_in_dim(
            total, lax.dynamic_slice_in_dim(total, start, window, 0) + grad_kvw[j], start, 0
        )
    return grad_q.reshape(rows, head_cols), normed, total


def per_device(heads_in, doc_units):
    section = lax.axis_index("sec")
    seq_place = lax.axis_index("seq")
    is_first = section == 0
    local_heads = heads_in[0]
    _, rows, cols = local_heads.shape
    half = cols // 2
    unit_count = rows // UNIT
    halo_units = MAX_DOC_UNITS - 1
    halo = halo_units * UNIT
    total_cols = cols * lax.axis_size("mp")

    keep_offset = section * half
    send_offset = (1 - section) * half
    sent = lax.dynamic_slice_in_dim(local_heads, send_offset, half, 2)
    kept = lax.dynamic_slice_in_dim(local_heads, keep_offset, half, 2)
    arrived = sec_swap(sent)
    key_value = jnp.where(is_first, kept, arrived)
    query_cot = jnp.where(is_first, arrived, kept)

    joined = jnp.concatenate([key_value[0], key_value[1]], axis=1)
    low, high = halo_swap(joined[:halo], joined[rows - halo :])
    near = jnp.concatenate([low, joined, high], axis=0)

    rel_starts, allowed = window_plan(doc_units, seq_place, unit_count, halo_units)

    def row_total(sums_pair):
        sums = jnp.stack(sums_pair)
        sums = sums + sec_swap(sums)
        sums = sums + lax.ppermute(sums, "mp", [(0, 1), (1, 0)])
        return sums[0], sums[1]

    grad_q, normed, total = attention_grads(
        query_cot[0],
        query_cot[1],
        near[:, :half],
        near[:, half:],
        rel_starts,
        allowed,
        row_total,
        total_cols,
    )
    from_left, from_right = halo_swap(
        total[:halo].astype(jnp.bfloat16), total[near.shape[0] - halo :].astype(jnp.bfloat16)
    )
    own = (
        total[halo : halo + rows]
        + jnp.pad(from_left.astype(jnp.float32), ((0, rows - halo), (0, 0)))
        + jnp.pad(from_right.astype(jnp.float32), ((rows - halo, 0), (0, 0)))
    )
    grad_k = own[:, :half].astype(jnp.bfloat16)
    grad_v = own[:, half:].astype(jnp.bfloat16)

    kv_pair = jnp.stack([grad_k, grad_v])
    qn_pair = jnp.stack([grad_q.astype(jnp.bfloat16), normed.astype(jnp.bfloat16)])
    back = sec_swap(jnp.where(is_first, qn_pair, kv_pair))
    result = jnp.where(
        is_first,
        jnp.concatenate([kv_pair, back], axis=2),
        jnp.concatenate([back, qn_pair], axis=2),
    )
    return result[None]


def solution(mesh):
    return jax.shard_map(
        per_device,
        mesh=mesh,
        in_specs=(P("sec", None, "seq", "mp"), P()),
        out_specs=P("sec", None, "seq", "mp"),
        check_vma=False,
    )
```

```python
import jax
import jax.numpy as jnp
from jax import lax
from jax.sharding import PartitionSpec as P

UNIT = 128
HEADS = 32
DH = 64
MAX_DOC_UNITS = 3


epsilon = 1e-06


def seq_shift(value, steps):
    count = lax.axis_size("seq")
    initial, last = (max(0, -steps), min(count, count - steps))
    return lax.ppermute(value, "seq", [(source, source + steps) for source in range(initial, last)])


def halo_swap(top, bottom):
    count = lax.axis_size("seq")
    even = lax.axis_index("seq") % 2 == 0
    inside = [(i, i ^ 1) for i in range(count) if (i ^ 1) < count]
    between = [(i, i + 1) for i in range(1, count - 1, 2)] + [(i + 1, i) for i in range(1, count - 1, 2)]
    within = lax.ppermute(jnp.where(even, bottom, top), "seq", inside)
    across = lax.ppermute(jnp.where(even, top, bottom), "seq", between)
    from_below = jnp.where(even, across, within)
    from_above = jnp.where(even, within, across)
    return from_below, from_above


def sec_swap(value):
    return lax.ppermute(value, "sec", [(0, 1), (1, 0)])


def window_plan(doc_units, seq_place, unit_count, halo_units):
    ends = jnp.cumsum(doc_units).astype(jnp.int32)
    first_unit = seq_place * unit_count
    query_units = first_unit + jnp.arange(unit_count, dtype=jnp.int32)

    def unit_doc(units):
        counted = jnp.sum((ends[None, :] <= units[:, None]).astype(jnp.int32), axis=1)
        return jnp.where(units < 0, jnp.int32(-1), counted)

    starts = jnp.max(
        jnp.where(ends[None, :] <= query_units[:, None], ends[None, :], 0), axis=1
    ).astype(jnp.int32)
    key_units = starts[:, None] + jnp.arange(MAX_DOC_UNITS, dtype=jnp.int32)[None, :]
    allowed = unit_doc(key_units.reshape(-1)).reshape(key_units.shape) == unit_doc(query_units)[:, None]
    return starts - (first_unit - halo_units), allowed


def attention_grads(queries, cotangent, near_keys, near_values, rel_starts, allowed, total_fn, total_cols):
    rows, head_cols = queries.shape
    heads = head_cols // DH
    unit_count = rows // UNIT
    window = MAX_DOC_UNITS * UNIT
    score_scale = DH ** (-0.5)

    def windows(near):
        pieces = [
            lax.dynamic_slice_in_dim(near, rel_starts[j] * UNIT, window, 0) for j in range(unit_count)
        ]
        return jnp.stack(pieces).reshape(unit_count, window, heads, DH)

    keys_w = windows(near_keys)
    values_w = windows(near_values)
    q4 = queries.reshape(unit_count, UNIT, heads, DH)
    cot_float = cotangent.astype(jnp.float32)

    mask = jnp.repeat(allowed, UNIT, axis=1)[:, None, None, :]
    scores = (
        jnp.einsum("jqhd,jkhd->jhqk", q4, keys_w, preferred_element_type=jnp.float32) * score_scale
    )
    scores = jnp.where(mask, scores, -jnp.inf)
    row_max = jnp.max(scores, axis=3, keepdims=True)
    expven = jnp.exp(scores - row_max)
    weights = expven / jnp.sum(expven, axis=3, keepdims=True)
    rounded = weights.astype(jnp.bfloat16)
    attended4 = jnp.einsum("jhqk,jkhd->jqhd", rounded, values_w, preferred_element_type=jnp.float32)
    attended = attended4.reshape(rows, head_cols)

    squares, crosses = total_fn(
        (jnp.sum(attended * attended, axis=1), jnp.sum(cot_float * attended, axis=1))
    )
    spread = jnp.sqrt(squares / total_cols + epsilon)
    normed = attended / spread[:, None]
    shared = crosses / total_cols / spread
    upstream = ((cot_float - normed * shared[:, None]) / spread[:, None]).astype(jnp.bfloat16)
    up4 = upstream.reshape(unit_count, UNIT, heads, DH)
    q_again, keys_again, up4 = lax.optimization_barrier((q4, keys_w, up4))
    scores = (
        jnp.einsum("jqhd,jkhd->jhqk", q_again, keys_again, preferred_element_type=jnp.float32)
        * score_scale
    )
    scores = jnp.where(mask, scores, -jnp.inf)
    expven = jnp.exp(scores - jnp.max(scores, axis=3, keepdims=True))
    weights = expven / jnp.sum(expven, axis=3, keepdims=True)
    rounded = weights.astype(jnp.bfloat16)

    delta = jnp.sum(up4.astype(jnp.float32) * attended4, axis=3)
    delta = jnp.transpose(delta, (0, 2, 1))[..., None]
    dprobs = jnp.einsum("jqhd,jkhd->jhqk", up4, values_w, preferred_element_type=jnp.float32)
    dscores = (weights * (dprobs - delta) * score_scale).astype(jnp.bfloat16)
    grad_q = jnp.einsum("jhqk,jkhd->jqhd", dscores, keys_w, preferred_element_type=jnp.float32)
    grad_kw = jnp.einsum("jhqk,jqhd->jkhd", dscores, q4, preferred_element_type=jnp.float32)
    grad_vw = jnp.einsum("jhqk,jqhd->jkhd", rounded, up4, preferred_element_type=jnp.float32)
    grad_kvw = jnp.concatenate(
        [grad_kw.reshape(unit_count, window, head_cols), grad_vw.reshape(unit_count, window, head_cols)],
        axis=2,
    )
    near_rows = near_keys.shape[0]
    total = jnp.zeros((near_rows, 2 * head_cols), jnp.float32)
    for j in range(unit_count):
        start = rel_starts[j] * UNIT
        total = lax.dynamic_update_slice_in_dim(
            total, lax.dynamic_slice_in_dim(total, start, window, 0) + grad_kvw[j], start, 0
        )
    return grad_q.reshape(rows, head_cols), normed, total


def per_device(heads_in, doc_units):
    section = lax.axis_index("sec")
    seq_place = lax.axis_index("seq")
    is_first = section == 0
    local_heads = heads_in[0]
    _, rows, cols = local_heads.shape
    half = cols // 2
    unit_count = rows // UNIT
    halo_units = MAX_DOC_UNITS - 1
    halo = halo_units * UNIT
    total_cols = cols * lax.axis_size("mp")

    keep_offset = section * half
    send_offset = (1 - section) * half
    sent = lax.dynamic_slice_in_dim(local_heads, send_offset, half, 2)
    kept = lax.dynamic_slice_in_dim(local_heads, keep_offset, half, 2)
    arrived = sec_swap(sent)
    key_value = jnp.where(is_first, kept, arrived)
    query_cot = jnp.where(is_first, arrived, kept)

    joined = jnp.concatenate([key_value[0], key_value[1]], axis=1)
    low, high = halo_swap(joined[:halo], joined[rows - halo :])
    near = jnp.concatenate([low, joined, high], axis=0)

    rel_starts, allowed = window_plan(doc_units, seq_place, unit_count, halo_units)

    def row_total(sums_pair):
        sums = jnp.stack(sums_pair)
        sums = sums + sec_swap(sums)
        sums = sums + lax.ppermute(sums, "mp", [(0, 1), (1, 0)])
        return sums[0], sums[1]

    grad_q, normed, total = attention_grads(
        query_cot[0],
        query_cot[1],
        near[:, :half],
        near[:, half:],
        rel_starts,
        allowed,
        row_total,
        total_cols,
    )
    from_left, from_right = halo_swap(
        total[:halo].astype(jnp.bfloat16), total[near.shape[0] - halo :].astype(jnp.bfloat16)
    )
    own = (
        total[halo : halo + rows]
        + jnp.pad(from_left.astype(jnp.float32), ((0, rows - halo), (0, 0)))
        + jnp.pad(from_right.astype(jnp.float32), ((rows - halo, 0), (0, 0)))
    )
    grad_k = own[:, :half].astype(jnp.bfloat16)
    grad_v = own[:, half:].astype(jnp.bfloat16)

    kv_pair = jnp.stack([grad_k, grad_v])
    qn_pair = jnp.stack([grad_q.astype(jnp.bfloat16), normed.astype(jnp.bfloat16)])
    back = sec_swap(jnp.where(is_first, qn_pair, kv_pair))
    result = jnp.where(
        is_first,
        jnp.concatenate([kv_pair, back], axis=2),
        jnp.concatenate([back, qn_pair], axis=2),
    )
    return result[None]


def solution(mesh):
    return jax.shard_map(
        per_device,
        mesh=mesh,
        in_specs=(P("sec", None, "seq", "mp"), P()),
        out_specs=P("sec", None, "seq", "mp"),
        check_vma=False,
    )
```

```python
import jax
import jax.numpy as jnp
from jax import lax
from jax.sharding import PartitionSpec as P

UNIT = 128
HEADS = 32
DH = 64
MAX_DOC_UNITS = 3


epsilon = 1e-06


def seq_shift(value, steps):
    count = lax.axis_size("seq")
    initial, last = (max(0, -steps), min(count, count - steps))
    return lax.ppermute(value, "seq", [(source, source + steps) for source in range(initial, last)])


def halo_swap(top, bottom):
    count = lax.axis_size("seq")
    even = lax.axis_index("seq") % 2 == 0
    inside = [(i, i ^ 1) for i in range(count) if (i ^ 1) < count]
    between = [(i, i + 1) for i in range(1, count - 1, 2)] + [(i + 1, i) for i in range(1, count - 1, 2)]
    within = lax.ppermute(jnp.where(even, bottom, top), "seq", inside)
    across = lax.ppermute(jnp.where(even, top, bottom), "seq", between)
    from_below = jnp.where(even, across, within)
    from_above = jnp.where(even, within, across)
    return from_below, from_above


def sec_swap(value):
    return lax.ppermute(value, "sec", [(0, 1), (1, 0)])


def window_plan(doc_units, seq_place, unit_count, halo_units):
    ends = jnp.cumsum(doc_units).astype(jnp.int32)
    first_unit = seq_place * unit_count
    query_units = first_unit + jnp.arange(unit_count, dtype=jnp.int32)

    def unit_doc(units):
        counted = jnp.sum((ends[None, :] <= units[:, None]).astype(jnp.int32), axis=1)
        return jnp.where(units < 0, jnp.int32(-1), counted)

    starts = jnp.max(
        jnp.where(ends[None, :] <= query_units[:, None], ends[None, :], 0), axis=1
    ).astype(jnp.int32)
    key_units = starts[:, None] + jnp.arange(MAX_DOC_UNITS, dtype=jnp.int32)[None, :]
    allowed = unit_doc(key_units.reshape(-1)).reshape(key_units.shape) == unit_doc(query_units)[:, None]
    return starts - (first_unit - halo_units), allowed


def attention_grads(queries, cotangent, near_keys, near_values, rel_starts, allowed, total_fn, total_cols):
    rows, head_cols = queries.shape
    heads = head_cols // DH
    unit_count = rows // UNIT
    window = MAX_DOC_UNITS * UNIT
    score_scale = DH ** (-0.5)

    def windows(near):
        pieces = [
            lax.dynamic_slice_in_dim(near, rel_starts[j] * UNIT, window, 0) for j in range(unit_count)
        ]
        return jnp.stack(pieces).reshape(unit_count, window, heads, DH)

    keys_w = windows(near_keys)
    values_w = windows(near_values)
    q4 = queries.reshape(unit_count, UNIT, heads, DH)
    cot_float = cotangent.astype(jnp.float32)

    mask = jnp.repeat(allowed, UNIT, axis=1)[:, None, None, :]
    scores = (
        jnp.einsum("jqhd,jkhd->jhqk", q4, keys_w, preferred_element_type=jnp.float32) * score_scale
    )
    scores = jnp.where(mask, scores, -jnp.inf)
    row_max = jnp.max(scores, axis=3, keepdims=True)
    expven = jnp.exp(scores - row_max)
    weights = expven / jnp.sum(expven, axis=3, keepdims=True)
    rounded = weights.astype(jnp.bfloat16)
    attended4 = jnp.einsum("jhqk,jkhd->jqhd", rounded, values_w, preferred_element_type=jnp.float32)
    attended = attended4.reshape(rows, head_cols)

    squares, crosses = total_fn(
        (jnp.sum(attended * attended, axis=1), jnp.sum(cot_float * attended, axis=1))
    )
    spread = jnp.sqrt(squares / total_cols + epsilon)
    normed = attended / spread[:, None]
    shared = crosses / total_cols / spread
    upstream = ((cot_float - normed * shared[:, None]) / spread[:, None]).astype(jnp.bfloat16)
    up4 = upstream.reshape(unit_count, UNIT, heads, DH)

    delta = jnp.sum(up4.astype(jnp.float32) * attended4, axis=3)
    delta = jnp.transpose(delta, (0, 2, 1))[..., None]
    dprobs = jnp.einsum("jqhd,jkhd->jhqk", up4, values_w, preferred_element_type=jnp.float32)
    dscores = (weights * (dprobs - delta) * score_scale).astype(jnp.bfloat16)
    grad_q = jnp.einsum("jhqk,jkhd->jqhd", dscores, keys_w, preferred_element_type=jnp.float32)
    grad_kw = jnp.einsum("jhqk,jqhd->jkhd", dscores, q4, preferred_element_type=jnp.float32)
    grad_vw = jnp.einsum("jhqk,jqhd->jkhd", rounded, up4, preferred_element_type=jnp.float32)
    grad_kvw = jnp.concatenate(
        [grad_kw.reshape(unit_count, window, head_cols), grad_vw.reshape(unit_count, window, head_cols)],
        axis=2,
    )
    near_rows = near_keys.shape[0]
    total = jnp.zeros((near_rows, 2 * head_cols), jnp.float32)
    for j in range(unit_count):
        start = rel_starts[j] * UNIT
        total = lax.dynamic_update_slice_in_dim(
            total, lax.dynamic_slice_in_dim(total, start, window, 0) + grad_kvw[j], start, 0
        )
    return grad_q.reshape(rows, head_cols), normed, total


def per_device(heads_in, doc_units):
    section = lax.axis_index("sec")
    seq_place = lax.axis_index("seq")
    is_first = section == 0
    local_heads = heads_in[0]
    _, rows, cols = local_heads.shape
    half = cols // 2
    unit_count = rows // UNIT
    halo_units = MAX_DOC_UNITS - 1
    halo = halo_units * UNIT
    total_cols = cols * lax.axis_size("mp")

    keep_offset = section * half
    send_offset = (1 - section) * half
    sent = lax.dynamic_slice_in_dim(local_heads, send_offset, half, 2)
    kept = lax.dynamic_slice_in_dim(local_heads, keep_offset, half, 2)
    arrived = sec_swap(sent)
    key_value = jnp.where(is_first, kept, arrived)
    query_cot = jnp.where(is_first, arrived, kept)

    joined = jnp.concatenate([key_value[0], key_value[1]], axis=1)
    low, high = halo_swap(joined[:halo], joined[rows - halo :])
    near = jnp.concatenate([low, joined, high], axis=0)

    rel_starts, allowed = window_plan(doc_units, seq_place, unit_count, halo_units)

    def row_total(sums_pair):
        sums = jnp.stack(sums_pair)
        sums = sums + sec_swap(sums)
        sums = sums + lax.ppermute(sums, "mp", [(0, 1), (1, 0)])
        return sums[0], sums[1]

    grad_q, normed, total = attention_grads(
        query_cot[0],
        query_cot[1],
        near[:, :half],
        near[:, half:],
        rel_starts,
        allowed,
        row_total,
        total_cols,
    )
    count = lax.axis_size("seq")
    even = seq_place % 2 == 0
    top = total[:halo].astype(jnp.bfloat16)
    bottom = total[near.shape[0] - halo :].astype(jnp.bfloat16)
    inside = [(i, i ^ 1) for i in range(count) if (i ^ 1) < count]
    between = [(i, i + 1) for i in range(1, count - 1, 2)] + [(i + 1, i) for i in range(1, count - 1, 2)]
    within = lax.ppermute(jnp.where(even, bottom, top), "seq", inside)
    across = lax.ppermute(jnp.where(even, top, bottom), "seq", between)
    middle = total[halo : halo + rows]
    early = rows - halo
    early_even = middle[rows - early :] + within[halo - early :].astype(jnp.float32)
    early_odd = middle[:early] + within[:early].astype(jnp.float32)
    early_own = jnp.where(even, early_even, early_odd).astype(jnp.bfloat16)
    qn_pair = jnp.stack([grad_q.astype(jnp.bfloat16), normed.astype(jnp.bfloat16)])
    early_kv = jnp.stack([early_own[:, :half], early_own[:, half:]])
    early_qn = jnp.where(even, qn_pair[:, rows - early :], qn_pair[:, :early])
    back_early = sec_swap(jnp.where(is_first, early_qn, early_kv))
    back_early, across = lax.optimization_barrier((back_early, across))
    from_left = jnp.where(even, across, within)
    from_right = jnp.where(even, within, across)
    own = (
        middle
        + jnp.pad(from_left.astype(jnp.float32), ((0, rows - halo), (0, 0)))
        + jnp.pad(from_right.astype(jnp.float32), ((rows - halo, 0), (0, 0)))
    )
    late_own = jnp.where(even, own[: rows - early], own[early:]).astype(jnp.bfloat16)
    grad_k = own[:, :half].astype(jnp.bfloat16)
    grad_v = own[:, half:].astype(jnp.bfloat16)
    kv_pair = jnp.stack([grad_k, grad_v])
    late_kv = jnp.stack([late_own[:, :half], late_own[:, half:]])
    late_qn = jnp.where(even, qn_pair[:, : rows - early], qn_pair[:, early:])
    back_late = sec_swap(jnp.where(is_first, late_qn, late_kv))
    back = jnp.where(
        even,
        jnp.concatenate([back_late, back_early], axis=1),
        jnp.concatenate([back_early, back_late], axis=1),
    )
    result = jnp.where(
        is_first,
        jnp.concatenate([kv_pair, back], axis=2),
        jnp.concatenate([back, qn_pair], axis=2),
    )
    return result[None]


def solution(mesh):
    return jax.shard_map(
        per_device,
        mesh=mesh,
        in_specs=(P("sec", None, "seq", "mp"), P()),
        out_specs=P("sec", None, "seq", "mp"),
        check_vma=False,
    )
```

```python
import jax
import jax.numpy as jnp
from jax import lax
from jax.sharding import PartitionSpec as P

UNIT = 128
HEADS = 32
DH = 64
MAX_DOC_UNITS = 3


epsilon = 1e-06


def seq_shift(value, steps):
    count = lax.axis_size("seq")
    initial, last = (max(0, -steps), min(count, count - steps))
    return lax.ppermute(value, "seq", [(source, source + steps) for source in range(initial, last)])


def halo_swap(top, bottom):
    count = lax.axis_size("seq")
    even = lax.axis_index("seq") % 2 == 0
    inside = [(i, i ^ 1) for i in range(count) if (i ^ 1) < count]
    between = [(i, i + 1) for i in range(1, count - 1, 2)] + [(i + 1, i) for i in range(1, count - 1, 2)]
    within = lax.ppermute(jnp.where(even, bottom, top), "seq", inside)
    across = lax.ppermute(jnp.where(even, top, bottom), "seq", between)
    from_below = jnp.where(even, across, within)
    from_above = jnp.where(even, within, across)
    return from_below, from_above


def sec_swap(value):
    return lax.ppermute(value, "sec", [(0, 1), (1, 0)])


def window_plan(doc_units, seq_place, unit_count, halo_units):
    ends = jnp.cumsum(doc_units).astype(jnp.int32)
    first_unit = seq_place * unit_count
    query_units = first_unit + jnp.arange(unit_count, dtype=jnp.int32)

    def unit_doc(units):
        counted = jnp.sum((ends[None, :] <= units[:, None]).astype(jnp.int32), axis=1)
        return jnp.where(units < 0, jnp.int32(-1), counted)

    starts = jnp.max(
        jnp.where(ends[None, :] <= query_units[:, None], ends[None, :], 0), axis=1
    ).astype(jnp.int32)
    key_units = starts[:, None] + jnp.arange(MAX_DOC_UNITS, dtype=jnp.int32)[None, :]
    allowed = unit_doc(key_units.reshape(-1)).reshape(key_units.shape) == unit_doc(query_units)[:, None]
    return starts - (first_unit - halo_units), allowed


def attention_grads(queries, cotangent, near_keys, near_values, rel_starts, allowed, total_fn, total_cols):
    rows, head_cols = queries.shape
    heads = head_cols // DH
    unit_count = rows // UNIT
    window = MAX_DOC_UNITS * UNIT
    score_scale = DH ** (-0.5)

    def windows(near):
        pieces = [
            lax.dynamic_slice_in_dim(near, rel_starts[j] * UNIT, window, 0) for j in range(unit_count)
        ]
        return jnp.stack(pieces).reshape(unit_count, window, heads, DH)

    keys_w = windows(near_keys)
    values_w = windows(near_values)
    q4 = queries.reshape(unit_count, UNIT, heads, DH)
    cot_float = cotangent.astype(jnp.float32)

    mask = jnp.repeat(allowed, UNIT, axis=1)[:, None, None, :]
    scores = (
        jnp.einsum("jqhd,jkhd->jhqk", q4, keys_w, preferred_element_type=jnp.float32) * score_scale
    )
    scores = jnp.where(mask, scores, -jnp.inf)
    row_max = jnp.max(scores, axis=3, keepdims=True)
    expven = jnp.exp(scores - row_max)
    weights = expven / jnp.sum(expven, axis=3, keepdims=True)
    rounded = weights.astype(jnp.bfloat16)
    attended4 = jnp.einsum("jhqk,jkhd->jqhd", rounded, values_w, preferred_element_type=jnp.float32)
    attended = attended4.reshape(rows, head_cols)

    squares, crosses = total_fn(
        (jnp.sum(attended * attended, axis=1), jnp.sum(cot_float * attended, axis=1))
    )
    spread = jnp.sqrt(squares / total_cols + epsilon)
    normed = attended / spread[:, None]
    shared = crosses / total_cols / spread
    upstream = ((cot_float - normed * shared[:, None]) / spread[:, None]).astype(jnp.bfloat16)
    up4 = upstream.reshape(unit_count, UNIT, heads, DH)

    delta = jnp.sum(up4.astype(jnp.float32) * attended4, axis=3)
    delta = jnp.transpose(delta, (0, 2, 1))[..., None]
    dprobs = jnp.einsum("jqhd,jkhd->jhqk", up4, values_w, preferred_element_type=jnp.float32)
    dscores = (weights * (dprobs - delta) * score_scale).astype(jnp.bfloat16)
    grad_q = jnp.einsum("jhqk,jkhd->jqhd", dscores, keys_w, preferred_element_type=jnp.float32)
    grad_kw = jnp.einsum("jhqk,jqhd->jkhd", dscores, q4, preferred_element_type=jnp.float32)
    grad_vw = jnp.einsum("jhqk,jqhd->jkhd", rounded, up4, preferred_element_type=jnp.float32)
    grad_kvw = jnp.concatenate(
        [grad_kw.reshape(unit_count, window, head_cols), grad_vw.reshape(unit_count, window, head_cols)],
        axis=2,
    )
    near_rows = near_keys.shape[0]
    total = jnp.zeros((near_rows, 2 * head_cols), jnp.float32)
    for j in range(unit_count):
        start = rel_starts[j] * UNIT
        total = lax.dynamic_update_slice_in_dim(
            total, lax.dynamic_slice_in_dim(total, start, window, 0) + grad_kvw[j], start, 0
        )
    return grad_q.reshape(rows, head_cols), normed, total


def per_device(heads_in, doc_units):
    section = lax.axis_index("sec")
    seq_place = lax.axis_index("seq")
    is_first = section == 0
    local_heads = heads_in[0]
    _, rows, cols = local_heads.shape
    half = cols // 2
    unit_count = rows // UNIT
    halo_units = MAX_DOC_UNITS - 1
    halo = halo_units * UNIT
    total_cols = cols * lax.axis_size("mp")

    keep_offset = section * half
    send_offset = (1 - section) * half
    even = seq_place % 2 == 0
    count = lax.axis_size("seq")
    inside = [(i, i ^ 1) for i in range(count) if (i ^ 1) < count]
    between = [(i, i + 1) for i in range(1, count - 1, 2)] + [(i + 1, i) for i in range(1, count - 1, 2)]
    sent = lax.dynamic_slice_in_dim(local_heads, send_offset, half, 2)
    kept = lax.dynamic_slice_in_dim(local_heads, keep_offset, half, 2)
    first_rows = jnp.where(even, sent[:, :halo], sent[:, rows - halo :])
    rest_rows = jnp.where(even, sent[:, halo:], sent[:, : rows - halo])
    arrived_first = sec_swap(first_rows)
    kept_first = jnp.where(even, kept[:, :halo], kept[:, rows - halo :])
    pair_first = jnp.where(is_first, kept_first, arrived_first)
    across = lax.ppermute(jnp.concatenate([pair_first[0], pair_first[1]], axis=1), "seq", between)
    arrived_rest = sec_swap(rest_rows)
    arrived_rest, across = lax.optimization_barrier((arrived_rest, across))
    arrived = jnp.where(
        even,
        jnp.concatenate([arrived_first, arrived_rest], axis=1),
        jnp.concatenate([arrived_rest, arrived_first], axis=1),
    )
    key_value = jnp.where(is_first, kept, arrived)
    query_cot = jnp.where(is_first, arrived, kept)

    joined = jnp.concatenate([key_value[0], key_value[1]], axis=1)
    within = lax.ppermute(jnp.where(even, joined[rows - halo :], joined[:halo]), "seq", inside)
    low = jnp.where(even, across, within)
    high = jnp.where(even, within, across)
    near = jnp.concatenate([low, joined, high], axis=0)

    rel_starts, allowed = window_plan(doc_units, seq_place, unit_count, halo_units)

    def row_total(sums_pair):
        sums = jnp.stack(sums_pair)
        sums = sums + sec_swap(sums)
        sums = sums + lax.ppermute(sums, "mp", [(0, 1), (1, 0)])
        return sums[0], sums[1]

    grad_q, normed, total = attention_grads(
        query_cot[0],
        query_cot[1],
        near[:, :half],
        near[:, half:],
        rel_starts,
        allowed,
        row_total,
        total_cols,
    )
    count = lax.axis_size("seq")
    even = seq_place % 2 == 0
    top = total[:halo].astype(jnp.bfloat16)
    bottom = total[near.shape[0] - halo :].astype(jnp.bfloat16)
    inside = [(i, i ^ 1) for i in range(count) if (i ^ 1) < count]
    between = [(i, i + 1) for i in range(1, count - 1, 2)] + [(i + 1, i) for i in range(1, count - 1, 2)]
    within = lax.ppermute(jnp.where(even, bottom, top), "seq", inside)
    across = lax.ppermute(jnp.where(even, top, bottom), "seq", between)
    middle = total[halo : halo + rows]
    early = rows - halo
    early_even = middle[rows - early :] + within[halo - early :].astype(jnp.float32)
    early_odd = middle[:early] + within[:early].astype(jnp.float32)
    early_own = jnp.where(even, early_even, early_odd).astype(jnp.bfloat16)
    qn_pair = jnp.stack([grad_q.astype(jnp.bfloat16), normed.astype(jnp.bfloat16)])
    early_kv = jnp.stack([early_own[:, :half], early_own[:, half:]])
    early_qn = jnp.where(even, qn_pair[:, rows - early :], qn_pair[:, :early])
    back_early = sec_swap(jnp.where(is_first, early_qn, early_kv))
    back_early, across = lax.optimization_barrier((back_early, across))
    from_left = jnp.where(even, across, within)
    from_right = jnp.where(even, within, across)
    own = (
        middle
        + jnp.pad(from_left.astype(jnp.float32), ((0, rows - halo), (0, 0)))
        + jnp.pad(from_right.astype(jnp.float32), ((rows - halo, 0), (0, 0)))
    )
    late_own = jnp.where(even, own[: rows - early], own[early:]).astype(jnp.bfloat16)
    grad_k = own[:, :half].astype(jnp.bfloat16)
    grad_v = own[:, half:].astype(jnp.bfloat16)
    kv_pair = jnp.stack([grad_k, grad_v])
    late_kv = jnp.stack([late_own[:, :half], late_own[:, half:]])
    late_qn = jnp.where(even, qn_pair[:, : rows - early], qn_pair[:, early:])
    back_late = sec_swap(jnp.where(is_first, late_qn, late_kv))
    back = jnp.where(
        even,
        jnp.concatenate([back_late, back_early], axis=1),
        jnp.concatenate([back_early, back_late], axis=1),
    )
    result = jnp.where(
        is_first,
        jnp.concatenate([kv_pair, back], axis=2),
        jnp.concatenate([back, qn_pair], axis=2),
    )
    return result[None]


def solution(mesh):
    return jax.shard_map(
        per_device,
        mesh=mesh,
        in_specs=(P("sec", None, "seq", "mp"), P()),
        out_specs=P("sec", None, "seq", "mp"),
        check_vma=False,
    )
```

```python
import jax
import jax.numpy as jnp
from jax import lax
from jax.sharding import PartitionSpec as P

UNIT = 128
HEADS = 32
DH = 64
MAX_DOC_UNITS = 3


epsilon = 1e-06


def seq_shift(value, steps):
    count = lax.axis_size("seq")
    initial, last = (max(0, -steps), min(count, count - steps))
    return lax.ppermute(value, "seq", [(source, source + steps) for source in range(initial, last)])


def halo_swap(top, bottom):
    count = lax.axis_size("seq")
    even = lax.axis_index("seq") % 2 == 0
    inside = [(i, i ^ 1) for i in range(count) if (i ^ 1) < count]
    between = [(i, i + 1) for i in range(1, count - 1, 2)] + [(i + 1, i) for i in range(1, count - 1, 2)]
    within = lax.ppermute(jnp.where(even, bottom, top), "seq", inside)
    across = lax.ppermute(jnp.where(even, top, bottom), "seq", between)
    from_below = jnp.where(even, across, within)
    from_above = jnp.where(even, within, across)
    return from_below, from_above


def sec_swap(value):
    return lax.ppermute(value, "sec", [(0, 1), (1, 0)])


def window_plan(doc_units, seq_place, unit_count, halo_units):
    ends = jnp.cumsum(doc_units).astype(jnp.int32)
    first_unit = seq_place * unit_count
    query_units = first_unit + jnp.arange(unit_count, dtype=jnp.int32)

    def unit_doc(units):
        counted = jnp.sum((ends[None, :] <= units[:, None]).astype(jnp.int32), axis=1)
        return jnp.where(units < 0, jnp.int32(-1), counted)

    starts = jnp.max(
        jnp.where(ends[None, :] <= query_units[:, None], ends[None, :], 0), axis=1
    ).astype(jnp.int32)
    key_units = starts[:, None] + jnp.arange(MAX_DOC_UNITS, dtype=jnp.int32)[None, :]
    allowed = unit_doc(key_units.reshape(-1)).reshape(key_units.shape) == unit_doc(query_units)[:, None]
    return starts - (first_unit - halo_units), allowed


def attention_grads(queries, cotangent, near_keys, near_values, rel_starts, allowed, total_fn, total_cols):
    rows, head_cols = queries.shape
    heads = head_cols // DH
    unit_count = rows // UNIT
    window = MAX_DOC_UNITS * UNIT
    score_scale = DH ** (-0.5)

    def windows(near):
        pieces = [
            lax.dynamic_slice_in_dim(near, rel_starts[j] * UNIT, window, 0) for j in range(unit_count)
        ]
        return jnp.stack(pieces).reshape(unit_count, window, heads, DH)

    keys_w = windows(near_keys)
    values_w = windows(near_values)
    q4 = queries.reshape(unit_count, UNIT, heads, DH)
    cot_float = cotangent.astype(jnp.float32)

    mask = jnp.repeat(allowed, UNIT, axis=1)[:, None, None, :]
    scores = (
        jnp.einsum("jqhd,jkhd->jhqk", q4, keys_w, preferred_element_type=jnp.float32) * score_scale
    )
    scores = jnp.where(mask, scores, -jnp.inf)
    row_max = jnp.max(scores, axis=3, keepdims=True)
    expven = jnp.exp(scores - row_max)
    weights = expven / jnp.sum(expven, axis=3, keepdims=True)
    rounded = weights.astype(jnp.bfloat16)
    attended4 = jnp.einsum("jhqk,jkhd->jqhd", rounded, values_w, preferred_element_type=jnp.float32)
    attended = attended4.reshape(rows, head_cols)

    squares, crosses = total_fn(
        (jnp.sum(attended * attended, axis=1), jnp.sum(cot_float * attended, axis=1))
    )
    spread = jnp.sqrt(squares / total_cols + epsilon)
    normed = attended / spread[:, None]
    shared = crosses / total_cols / spread
    upstream = ((cot_float - normed * shared[:, None]) / spread[:, None]).astype(jnp.bfloat16)
    up4 = upstream.reshape(unit_count, UNIT, heads, DH)

    delta = jnp.sum(up4.astype(jnp.float32) * attended4, axis=3)
    delta = jnp.transpose(delta, (0, 2, 1))[..., None]
    dprobs = jnp.einsum("jqhd,jkhd->jhqk", up4, values_w, preferred_element_type=jnp.float32)
    dscores = (weights * (dprobs - delta) * score_scale).astype(jnp.bfloat16)
    grad_q = jnp.einsum("jhqk,jkhd->jqhd", dscores, keys_w, preferred_element_type=jnp.float32)
    grad_kw = jnp.einsum("jhqk,jqhd->jkhd", dscores, q4, preferred_element_type=jnp.float32)
    grad_vw = jnp.einsum("jhqk,jqhd->jkhd", rounded, up4, preferred_element_type=jnp.float32)
    grad_kvw = jnp.concatenate(
        [grad_kw.reshape(unit_count, window, head_cols), grad_vw.reshape(unit_count, window, head_cols)],
        axis=2,
    )
    near_rows = near_keys.shape[0]
    total = jnp.zeros((near_rows, 2 * head_cols), jnp.float32)
    for j in range(unit_count):
        start = rel_starts[j] * UNIT
        total = lax.dynamic_update_slice_in_dim(
            total, lax.dynamic_slice_in_dim(total, start, window, 0) + grad_kvw[j], start, 0
        )
    return grad_q.reshape(rows, head_cols), normed, total


def per_device(heads_in, doc_units):
    section = lax.axis_index("sec")
    seq_place = lax.axis_index("seq")
    is_first = section == 0
    local_heads = heads_in[0]
    _, rows, cols = local_heads.shape
    half = cols // 2
    unit_count = rows // UNIT
    halo_units = MAX_DOC_UNITS - 1
    halo = halo_units * UNIT
    total_cols = cols * lax.axis_size("mp")

    keep_offset = section * half
    send_offset = (1 - section) * half
    even = seq_place % 2 == 0
    count = lax.axis_size("seq")
    inside = [(i, i ^ 1) for i in range(count) if (i ^ 1) < count]
    between = [(i, i + 1) for i in range(1, count - 1, 2)] + [(i + 1, i) for i in range(1, count - 1, 2)]
    sent = lax.dynamic_slice_in_dim(local_heads, send_offset, half, 2)
    kept = lax.dynamic_slice_in_dim(local_heads, keep_offset, half, 2)
    first_rows = jnp.where(even, sent[:, :halo], sent[:, rows - halo :])
    rest_rows = jnp.where(even, sent[:, halo:], sent[:, : rows - halo])
    arrived_first = sec_swap(first_rows)
    rest_rows, arrived_first = lax.optimization_barrier((rest_rows, arrived_first))
    kept_first = jnp.where(even, kept[:, :halo], kept[:, rows - halo :])
    pair_first = jnp.where(is_first, kept_first, arrived_first)
    across = lax.ppermute(jnp.concatenate([pair_first[0], pair_first[1]], axis=1), "seq", between)
    arrived_rest = sec_swap(rest_rows)
    arrived_rest, across = lax.optimization_barrier((arrived_rest, across))
    arrived = jnp.where(
        even,
        jnp.concatenate([arrived_first, arrived_rest], axis=1),
        jnp.concatenate([arrived_rest, arrived_first], axis=1),
    )
    key_value = jnp.where(is_first, kept, arrived)
    query_cot = jnp.where(is_first, arrived, kept)

    joined = jnp.concatenate([key_value[0], key_value[1]], axis=1)
    within = lax.ppermute(jnp.where(even, joined[rows - halo :], joined[:halo]), "seq", inside)
    low = jnp.where(even, across, within)
    high = jnp.where(even, within, across)
    near = jnp.concatenate([low, joined, high], axis=0)

    rel_starts, allowed = window_plan(doc_units, seq_place, unit_count, halo_units)

    def row_total(sums_pair):
        sums = jnp.stack(sums_pair)
        sums = sums + sec_swap(sums)
        sums = sums + lax.ppermute(sums, "mp", [(0, 1), (1, 0)])
        return sums[0], sums[1]

    grad_q, normed, total = attention_grads(
        query_cot[0],
        query_cot[1],
        near[:, :half],
        near[:, half:],
        rel_starts,
        allowed,
        row_total,
        total_cols,
    )
    count = lax.axis_size("seq")
    even = seq_place % 2 == 0
    top = total[:halo].astype(jnp.bfloat16)
    bottom = total[near.shape[0] - halo :].astype(jnp.bfloat16)
    inside = [(i, i ^ 1) for i in range(count) if (i ^ 1) < count]
    between = [(i, i + 1) for i in range(1, count - 1, 2)] + [(i + 1, i) for i in range(1, count - 1, 2)]
    within = lax.ppermute(jnp.where(even, bottom, top), "seq", inside)
    across = lax.ppermute(jnp.where(even, top, bottom), "seq", between)
    middle = total[halo : halo + rows]
    early = rows - halo
    early_even = middle[rows - early :] + within[halo - early :].astype(jnp.float32)
    early_odd = middle[:early] + within[:early].astype(jnp.float32)
    early_own = jnp.where(even, early_even, early_odd).astype(jnp.bfloat16)
    qn_pair = jnp.stack([grad_q.astype(jnp.bfloat16), normed.astype(jnp.bfloat16)])
    early_kv = jnp.stack([early_own[:, :half], early_own[:, half:]])
    early_qn = jnp.where(even, qn_pair[:, rows - early :], qn_pair[:, :early])
    back_early = sec_swap(jnp.where(is_first, early_qn, early_kv))
    back_early, across = lax.optimization_barrier((back_early, across))
    from_left = jnp.where(even, across, within)
    from_right = jnp.where(even, within, across)
    own = (
        middle
        + jnp.pad(from_left.astype(jnp.float32), ((0, rows - halo), (0, 0)))
        + jnp.pad(from_right.astype(jnp.float32), ((rows - halo, 0), (0, 0)))
    )
    late_own = jnp.where(even, own[: rows - early], own[early:]).astype(jnp.bfloat16)
    grad_k = own[:, :half].astype(jnp.bfloat16)
    grad_v = own[:, half:].astype(jnp.bfloat16)
    kv_pair = jnp.stack([grad_k, grad_v])
    late_kv = jnp.stack([late_own[:, :half], late_own[:, half:]])
    late_qn = jnp.where(even, qn_pair[:, : rows - early], qn_pair[:, early:])
    back_late = sec_swap(jnp.where(is_first, late_qn, late_kv))
    back = jnp.where(
        even,
        jnp.concatenate([back_late, back_early], axis=1),
        jnp.concatenate([back_early, back_late], axis=1),
    )
    result = jnp.where(
        is_first,
        jnp.concatenate([kv_pair, back], axis=2),
        jnp.concatenate([back, qn_pair], axis=2),
    )
    return result[None]


def solution(mesh):
    return jax.shard_map(
        per_device,
        mesh=mesh,
        in_specs=(P("sec", None, "seq", "mp"), P()),
        out_specs=P("sec", None, "seq", "mp"),
        check_vma=False,
    )
```

```python
import jax
import jax.numpy as jnp
from jax import lax
from jax.sharding import PartitionSpec as P

UNIT = 128
HEADS = 32
DH = 64
MAX_DOC_UNITS = 3


epsilon = 1e-06


def seq_shift(value, steps):
    count = lax.axis_size("seq")
    initial, last = (max(0, -steps), min(count, count - steps))
    return lax.ppermute(value, "seq", [(source, source + steps) for source in range(initial, last)])


def halo_swap(top, bottom):
    count = lax.axis_size("seq")
    even = lax.axis_index("seq") % 2 == 0
    inside = [(i, i ^ 1) for i in range(count) if (i ^ 1) < count]
    between = [(i, i + 1) for i in range(1, count - 1, 2)] + [(i + 1, i) for i in range(1, count - 1, 2)]
    within = lax.ppermute(jnp.where(even, bottom, top), "seq", inside)
    across = lax.ppermute(jnp.where(even, top, bottom), "seq", between)
    from_below = jnp.where(even, across, within)
    from_above = jnp.where(even, within, across)
    return from_below, from_above


def sec_swap(value):
    return lax.ppermute(value, "sec", [(0, 1), (1, 0)])


def window_plan(doc_units, seq_place, unit_count, halo_units):
    ends = jnp.cumsum(doc_units).astype(jnp.int32)
    first_unit = seq_place * unit_count
    query_units = first_unit + jnp.arange(unit_count, dtype=jnp.int32)

    def unit_doc(units):
        counted = jnp.sum((ends[None, :] <= units[:, None]).astype(jnp.int32), axis=1)
        return jnp.where(units < 0, jnp.int32(-1), counted)

    starts = jnp.max(
        jnp.where(ends[None, :] <= query_units[:, None], ends[None, :], 0), axis=1
    ).astype(jnp.int32)
    key_units = starts[:, None] + jnp.arange(MAX_DOC_UNITS, dtype=jnp.int32)[None, :]
    allowed = unit_doc(key_units.reshape(-1)).reshape(key_units.shape) == unit_doc(query_units)[:, None]
    return starts - (first_unit - halo_units), allowed


def attention_grads(queries, cotangent, near_keys, near_values, rel_starts, allowed, total_fn, total_cols):
    rows, head_cols = queries.shape
    heads = head_cols // DH
    unit_count = rows // UNIT
    window = MAX_DOC_UNITS * UNIT
    score_scale = DH ** (-0.5)

    def windows(near):
        pieces = [
            lax.dynamic_slice_in_dim(near, rel_starts[j] * UNIT, window, 0) for j in range(unit_count)
        ]
        return jnp.stack(pieces).reshape(unit_count, window, heads, DH)

    keys_w = windows(near_keys)
    values_w = windows(near_values)
    q4 = queries.reshape(unit_count, UNIT, heads, DH)
    cot_float = cotangent.astype(jnp.float32)

    mask = jnp.repeat(allowed, UNIT, axis=1)[:, None, None, :]
    scores = (
        jnp.einsum("jqhd,jkhd->jhqk", q4, keys_w, preferred_element_type=jnp.float32) * score_scale
    )
    scores = jnp.where(mask, scores, -jnp.inf)
    row_max = jnp.max(scores, axis=3, keepdims=True)
    expven = jnp.exp(scores - row_max)
    weights = expven / jnp.sum(expven, axis=3, keepdims=True)
    rounded = weights.astype(jnp.bfloat16)
    attended4 = jnp.einsum("jhqk,jkhd->jqhd", rounded, values_w, preferred_element_type=jnp.float32)
    attended = attended4.reshape(rows, head_cols)

    squares, crosses = total_fn(
        (jnp.sum(attended * attended, axis=1), jnp.sum(cot_float * attended, axis=1))
    )
    spread = jnp.sqrt(squares / total_cols + epsilon)
    normed = attended / spread[:, None]
    shared = crosses / total_cols / spread
    upstream = ((cot_float - normed * shared[:, None]) / spread[:, None]).astype(jnp.bfloat16)
    up4 = upstream.reshape(unit_count, UNIT, heads, DH)

    delta = jnp.sum(up4.astype(jnp.float32) * attended4, axis=3)
    delta = jnp.transpose(delta, (0, 2, 1))[..., None]
    dprobs = jnp.einsum("jqhd,jkhd->jhqk", up4, values_w, preferred_element_type=jnp.float32)
    dscores = (weights * (dprobs - delta) * score_scale).astype(jnp.bfloat16)
    grad_q = jnp.einsum("jhqk,jkhd->jqhd", dscores, keys_w, preferred_element_type=jnp.float32)
    grad_kw = jnp.einsum("jhqk,jqhd->jkhd", dscores, q4, preferred_element_type=jnp.float32)
    grad_vw = jnp.einsum("jhqk,jqhd->jkhd", rounded, up4, preferred_element_type=jnp.float32)
    grad_kvw = jnp.concatenate(
        [grad_kw.reshape(unit_count, window, head_cols), grad_vw.reshape(unit_count, window, head_cols)],
        axis=2,
    )
    near_rows = near_keys.shape[0]
    total = jnp.zeros((near_rows, 2 * head_cols), jnp.float32)
    for j in range(unit_count):
        start = rel_starts[j] * UNIT
        total = lax.dynamic_update_slice_in_dim(
            total, lax.dynamic_slice_in_dim(total, start, window, 0) + grad_kvw[j], start, 0
        )
    return grad_q.reshape(rows, head_cols), normed, total


def per_device(heads_in, doc_units):
    section = lax.axis_index("sec")
    seq_place = lax.axis_index("seq")
    is_first = section == 0
    local_heads = heads_in[0]
    _, rows, cols = local_heads.shape
    half = cols // 2
    unit_count = rows // UNIT
    halo_units = MAX_DOC_UNITS - 1
    halo = halo_units * UNIT
    total_cols = cols * lax.axis_size("mp")

    first_half = local_heads[:, :, :half]
    second_half = local_heads[:, :, half:]
    sent = jnp.where(is_first, second_half, first_half)
    kept = jnp.where(is_first, first_half, second_half)
    arrived = sec_swap(sent)
    key_value = jnp.where(is_first, kept, arrived)
    query_cot = jnp.where(is_first, arrived, kept)

    joined = jnp.concatenate([key_value[0], key_value[1]], axis=1)
    low, high = halo_swap(joined[:halo], joined[rows - halo :])
    near = jnp.concatenate([low, joined, high], axis=0)

    rel_starts, allowed = window_plan(doc_units, seq_place, unit_count, halo_units)

    def row_total(sums_pair):
        sums = jnp.stack(sums_pair)
        sums = sums + sec_swap(sums)
        sums = sums + lax.ppermute(sums, "mp", [(0, 1), (1, 0)])
        return sums[0], sums[1]

    grad_q, normed, total = attention_grads(
        query_cot[0],
        query_cot[1],
        near[:, :half],
        near[:, half:],
        rel_starts,
        allowed,
        row_total,
        total_cols,
    )
    count = lax.axis_size("seq")
    even = seq_place % 2 == 0
    top = total[:halo].astype(jnp.bfloat16)
    bottom = total[near.shape[0] - halo :].astype(jnp.bfloat16)
    inside = [(i, i ^ 1) for i in range(count) if (i ^ 1) < count]
    between = [(i, i + 1) for i in range(1, count - 1, 2)] + [(i + 1, i) for i in range(1, count - 1, 2)]
    within = lax.ppermute(jnp.where(even, bottom, top), "seq", inside)
    across = lax.ppermute(jnp.where(even, top, bottom), "seq", between)
    middle = total[halo : halo + rows]
    early = rows - halo
    early_even = middle[rows - early :] + within[halo - early :].astype(jnp.float32)
    early_odd = middle[:early] + within[:early].astype(jnp.float32)
    early_own = jnp.where(even, early_even, early_odd).astype(jnp.bfloat16)
    qn_pair = jnp.stack([grad_q.astype(jnp.bfloat16), normed.astype(jnp.bfloat16)])
    early_kv = jnp.stack([early_own[:, :half], early_own[:, half:]])
    early_qn = jnp.where(even, qn_pair[:, rows - early :], qn_pair[:, :early])
    back_early = sec_swap(jnp.where(is_first, early_qn, early_kv))
    back_early, across = lax.optimization_barrier((back_early, across))
    from_left = jnp.where(even, across, within)
    from_right = jnp.where(even, within, across)
    own = (
        middle
        + jnp.pad(from_left.astype(jnp.float32), ((0, rows - halo), (0, 0)))
        + jnp.pad(from_right.astype(jnp.float32), ((rows - halo, 0), (0, 0)))
    )
    late_own = jnp.where(even, own[: rows - early], own[early:]).astype(jnp.bfloat16)
    grad_k = own[:, :half].astype(jnp.bfloat16)
    grad_v = own[:, half:].astype(jnp.bfloat16)
    kv_pair = jnp.stack([grad_k, grad_v])
    late_kv = jnp.stack([late_own[:, :half], late_own[:, half:]])
    late_qn = jnp.where(even, qn_pair[:, : rows - early], qn_pair[:, early:])
    back_late = sec_swap(jnp.where(is_first, late_qn, late_kv))
    back = jnp.where(
        even,
        jnp.concatenate([back_late, back_early], axis=1),
        jnp.concatenate([back_early, back_late], axis=1),
    )
    result = jnp.where(
        is_first,
        jnp.concatenate([kv_pair, back], axis=2),
        jnp.concatenate([back, qn_pair], axis=2),
    )
    return result[None]


def solution(mesh):
    return jax.shard_map(
        per_device,
        mesh=mesh,
        in_specs=(P("sec", None, "seq", "mp"), P()),
        out_specs=P("sec", None, "seq", "mp"),
        check_vma=False,
    )
```

```python
import jax
import jax.numpy as jnp
from jax import lax
from jax.sharding import PartitionSpec as P

UNIT = 128
HEADS = 32
DH = 64
MAX_DOC_UNITS = 3


epsilon = 1e-06


def seq_shift(value, steps):
    count = lax.axis_size("seq")
    initial, last = (max(0, -steps), min(count, count - steps))
    return lax.ppermute(value, "seq", [(source, source + steps) for source in range(initial, last)])


def halo_swap(top, bottom):
    count = lax.axis_size("seq")
    even = lax.axis_index("seq") % 2 == 0
    inside = [(i, i ^ 1) for i in range(count) if (i ^ 1) < count]
    between = [(i, i + 1) for i in range(1, count - 1, 2)] + [(i + 1, i) for i in range(1, count - 1, 2)]
    within = lax.ppermute(jnp.where(even, bottom, top), "seq", inside)
    across = lax.ppermute(jnp.where(even, top, bottom), "seq", between)
    from_below = jnp.where(even, across, within)
    from_above = jnp.where(even, within, across)
    return from_below, from_above


def sec_swap(value):
    return lax.ppermute(value, "sec", [(0, 1), (1, 0)])


def window_plan(doc_units, seq_place, unit_count, halo_units):
    ends = jnp.cumsum(doc_units).astype(jnp.int32)
    first_unit = seq_place * unit_count
    query_units = first_unit + jnp.arange(unit_count, dtype=jnp.int32)

    def unit_doc(units):
        counted = jnp.sum((ends[None, :] <= units[:, None]).astype(jnp.int32), axis=1)
        return jnp.where(units < 0, jnp.int32(-1), counted)

    starts = jnp.max(
        jnp.where(ends[None, :] <= query_units[:, None], ends[None, :], 0), axis=1
    ).astype(jnp.int32)
    key_units = starts[:, None] + jnp.arange(MAX_DOC_UNITS, dtype=jnp.int32)[None, :]
    allowed = unit_doc(key_units.reshape(-1)).reshape(key_units.shape) == unit_doc(query_units)[:, None]
    return starts - (first_unit - halo_units), allowed


def attention_grads(queries, cotangent, near_keys, near_values, rel_starts, allowed, total_fn, total_cols):
    rows, head_cols = queries.shape
    heads = head_cols // DH
    unit_count = rows // UNIT
    window = MAX_DOC_UNITS * UNIT
    score_scale = DH ** (-0.5)

    def windows(near):
        pieces = [
            lax.dynamic_slice_in_dim(near, rel_starts[j] * UNIT, window, 0) for j in range(unit_count)
        ]
        return jnp.stack(pieces).reshape(unit_count, window, heads, DH)

    keys_w = windows(near_keys)
    values_w = windows(near_values)
    q4 = queries.reshape(unit_count, UNIT, heads, DH)
    cot_float = cotangent.astype(jnp.float32)

    mask = jnp.repeat(allowed, UNIT, axis=1)[:, None, None, :]
    scores = (
        jnp.einsum("jqhd,jkhd->jhqk", q4, keys_w, preferred_element_type=jnp.float32) * score_scale
    )
    scores = jnp.where(mask, scores, -jnp.inf)
    row_max = jnp.max(scores, axis=3, keepdims=True)
    expven = jnp.exp(scores - row_max)
    weights = expven / jnp.sum(expven, axis=3, keepdims=True)
    rounded = weights.astype(jnp.bfloat16)
    attended4 = jnp.einsum("jhqk,jkhd->jqhd", rounded, values_w, preferred_element_type=jnp.float32)
    attended = attended4.reshape(rows, head_cols)

    squares, crosses = total_fn(
        (jnp.sum(attended * attended, axis=1), jnp.sum(cot_float * attended, axis=1))
    )
    spread = jnp.sqrt(squares / total_cols + epsilon)
    normed = attended / spread[:, None]
    shared = crosses / total_cols / spread
    upstream = ((cot_float - normed * shared[:, None]) / spread[:, None]).astype(jnp.bfloat16)
    up4 = upstream.reshape(unit_count, UNIT, heads, DH)

    delta = jnp.sum(up4.astype(jnp.float32) * attended4, axis=3)
    delta = jnp.transpose(delta, (0, 2, 1))[..., None]
    dprobs = jnp.einsum("jqhd,jkhd->jhqk", up4, values_w, preferred_element_type=jnp.float32)
    dscores = (weights * (dprobs - delta) * score_scale).astype(jnp.bfloat16)
    grad_q = jnp.einsum("jhqk,jkhd->jqhd", dscores, keys_w, preferred_element_type=jnp.float32)
    grad_kw = jnp.einsum("jhqk,jqhd->jkhd", dscores, q4, preferred_element_type=jnp.float32)
    grad_vw = jnp.einsum("jhqk,jqhd->jkhd", rounded, up4, preferred_element_type=jnp.float32)
    grad_kvw = jnp.concatenate(
        [grad_kw.reshape(unit_count, window, head_cols), grad_vw.reshape(unit_count, window, head_cols)],
        axis=2,
    )
    near_rows = near_keys.shape[0]
    total = jnp.zeros((near_rows, 2 * head_cols), jnp.float32)
    for j in range(unit_count):
        start = rel_starts[j] * UNIT
        total = lax.dynamic_update_slice_in_dim(
            total, lax.dynamic_slice_in_dim(total, start, window, 0) + grad_kvw[j], start, 0
        )
    return grad_q.reshape(rows, head_cols), normed, total


def per_device(heads_in, doc_units):
    section = lax.axis_index("sec")
    seq_place = lax.axis_index("seq")
    is_first = section == 0
    local_heads = heads_in[0]
    _, rows, cols = local_heads.shape
    half = cols // 2
    unit_count = rows // UNIT
    halo_units = MAX_DOC_UNITS - 1
    halo = halo_units * UNIT
    total_cols = cols * lax.axis_size("mp")

    keep_offset = section * half
    send_offset = (1 - section) * half
    sent = lax.dynamic_slice_in_dim(local_heads, send_offset, half, 2)
    kept = lax.dynamic_slice_in_dim(local_heads, keep_offset, half, 2)
    arrived = sec_swap(sent)
    key_value = jnp.where(is_first, kept, arrived)
    query_cot = jnp.where(is_first, arrived, kept)

    joined = jnp.concatenate([key_value[0], key_value[1]], axis=1)
    low, high = halo_swap(joined[:halo], joined[rows - halo :])
    near = jnp.concatenate([low, joined, high], axis=0)

    rel_starts, allowed = window_plan(doc_units, seq_place, unit_count, halo_units)

    def row_total(sums_pair):
        sums = jnp.stack(sums_pair)
        sums = sums + lax.ppermute(sums, "mp", [(0, 1), (1, 0)])
        sums = sums + sec_swap(sums)
        return sums[0], sums[1]

    grad_q, normed, total = attention_grads(
        query_cot[0],
        query_cot[1],
        near[:, :half],
        near[:, half:],
        rel_starts,
        allowed,
        row_total,
        total_cols,
    )
    count = lax.axis_size("seq")
    even = seq_place % 2 == 0
    top = total[:halo].astype(jnp.bfloat16)
    bottom = total[near.shape[0] - halo :].astype(jnp.bfloat16)
    inside = [(i, i ^ 1) for i in range(count) if (i ^ 1) < count]
    between = [(i, i + 1) for i in range(1, count - 1, 2)] + [(i + 1, i) for i in range(1, count - 1, 2)]
    within = lax.ppermute(jnp.where(even, bottom, top), "seq", inside)
    across = lax.ppermute(jnp.where(even, top, bottom), "seq", between)
    middle = total[halo : halo + rows]
    early = rows - halo
    early_even = middle[rows - early :] + within[halo - early :].astype(jnp.float32)
    early_odd = middle[:early] + within[:early].astype(jnp.float32)
    early_own = jnp.where(even, early_even, early_odd).astype(jnp.bfloat16)
    qn_pair = jnp.stack([grad_q.astype(jnp.bfloat16), normed.astype(jnp.bfloat16)])
    early_kv = jnp.stack([early_own[:, :half], early_own[:, half:]])
    early_qn = jnp.where(even, qn_pair[:, rows - early :], qn_pair[:, :early])
    back_early = sec_swap(jnp.where(is_first, early_qn, early_kv))
    back_early, across = lax.optimization_barrier((back_early, across))
    from_left = jnp.where(even, across, within)
    from_right = jnp.where(even, within, across)
    own = (
        middle
        + jnp.pad(from_left.astype(jnp.float32), ((0, rows - halo), (0, 0)))
        + jnp.pad(from_right.astype(jnp.float32), ((rows - halo, 0), (0, 0)))
    )
    late_own = jnp.where(even, own[: rows - early], own[early:]).astype(jnp.bfloat16)
    grad_k = own[:, :half].astype(jnp.bfloat16)
    grad_v = own[:, half:].astype(jnp.bfloat16)
    kv_pair = jnp.stack([grad_k, grad_v])
    late_kv = jnp.stack([late_own[:, :half], late_own[:, half:]])
    late_qn = jnp.where(even, qn_pair[:, : rows - early], qn_pair[:, early:])
    back_late = sec_swap(jnp.where(is_first, late_qn, late_kv))
    back = jnp.where(
        even,
        jnp.concatenate([back_late, back_early], axis=1),
        jnp.concatenate([back_early, back_late], axis=1),
    )
    result = jnp.where(
        is_first,
        jnp.concatenate([kv_pair, back], axis=2),
        jnp.concatenate([back, qn_pair], axis=2),
    )
    return result[None]


def solution(mesh):
    return jax.shard_map(
        per_device,
        mesh=mesh,
        in_specs=(P("sec", None, "seq", "mp"), P()),
        out_specs=P("sec", None, "seq", "mp"),
        check_vma=False,
    )
```

```python
import jax
import jax.numpy as jnp
from jax import lax
from jax.sharding import PartitionSpec as P

UNIT = 128
HEADS = 32
DH = 64
MAX_DOC_UNITS = 3


epsilon = 1e-06


def seq_shift(value, steps):
    count = lax.axis_size("seq")
    initial, last = (max(0, -steps), min(count, count - steps))
    return lax.ppermute(value, "seq", [(source, source + steps) for source in range(initial, last)])


def halo_swap(top, bottom):
    count = lax.axis_size("seq")
    even = lax.axis_index("seq") % 2 == 0
    inside = [(i, i ^ 1) for i in range(count) if (i ^ 1) < count]
    between = [(i, i + 1) for i in range(1, count - 1, 2)] + [(i + 1, i) for i in range(1, count - 1, 2)]
    within = lax.ppermute(jnp.where(even, bottom, top), "seq", inside)
    across = lax.ppermute(jnp.where(even, top, bottom), "seq", between)
    from_below = jnp.where(even, across, within)
    from_above = jnp.where(even, within, across)
    return from_below, from_above


def sec_swap(value):
    return lax.ppermute(value, "sec", [(0, 1), (1, 0)])


def window_plan(doc_units, seq_place, unit_count, halo_units):
    ends = jnp.cumsum(doc_units).astype(jnp.int32)
    first_unit = seq_place * unit_count
    query_units = first_unit + jnp.arange(unit_count, dtype=jnp.int32)

    def unit_doc(units):
        counted = jnp.sum((ends[None, :] <= units[:, None]).astype(jnp.int32), axis=1)
        return jnp.where(units < 0, jnp.int32(-1), counted)

    starts = jnp.max(
        jnp.where(ends[None, :] <= query_units[:, None], ends[None, :], 0), axis=1
    ).astype(jnp.int32)
    key_units = starts[:, None] + jnp.arange(MAX_DOC_UNITS, dtype=jnp.int32)[None, :]
    allowed = unit_doc(key_units.reshape(-1)).reshape(key_units.shape) == unit_doc(query_units)[:, None]
    return starts - (first_unit - halo_units), allowed


def attention_grads(queries, cotangent, near_keys, near_values, rel_starts, allowed, total_fn, total_cols):
    rows, head_cols = queries.shape
    heads = head_cols // DH
    unit_count = rows // UNIT
    window = MAX_DOC_UNITS * UNIT
    score_scale = DH ** (-0.5)

    def windows(near):
        pieces = [
            lax.dynamic_slice_in_dim(near, rel_starts[j] * UNIT, window, 0) for j in range(unit_count)
        ]
        return jnp.stack(pieces).reshape(unit_count, window, heads, DH)

    keys_w = windows(near_keys)
    values_w = windows(near_values)
    q4 = queries.reshape(unit_count, UNIT, heads, DH)
    cot_float = cotangent.astype(jnp.float32)

    mask = jnp.repeat(allowed, UNIT, axis=1)[:, None, None, :]
    scores = (
        jnp.einsum("jqhd,jkhd->jhqk", q4, keys_w, preferred_element_type=jnp.float32) * score_scale
    )
    scores = jnp.where(mask, scores, -jnp.inf)
    row_max = jnp.max(scores, axis=3, keepdims=True)
    expven = jnp.exp(scores - row_max)
    weights = expven / jnp.sum(expven, axis=3, keepdims=True)
    rounded = weights.astype(jnp.bfloat16)
    attended4 = jnp.einsum("jhqk,jkhd->jqhd", rounded, values_w, preferred_element_type=jnp.float32)
    attended = attended4.reshape(rows, head_cols)

    squares, crosses = total_fn(
        (jnp.sum(attended * attended, axis=1), jnp.sum(cot_float * attended, axis=1))
    )
    spread = jnp.sqrt(squares / total_cols + epsilon)
    normed = attended / spread[:, None]
    shared = crosses / total_cols / spread
    upstream = ((cot_float - normed * shared[:, None]) / spread[:, None]).astype(jnp.bfloat16)
    up4 = upstream.reshape(unit_count, UNIT, heads, DH)

    delta = jnp.sum(up4.astype(jnp.float32) * attended4, axis=3)
    delta = jnp.transpose(delta, (0, 2, 1))[..., None]
    dprobs = jnp.einsum("jqhd,jkhd->jhqk", up4, values_w, preferred_element_type=jnp.float32)
    dscores = (weights * (dprobs - delta) * score_scale).astype(jnp.bfloat16)
    grad_q = jnp.einsum("jhqk,jkhd->jqhd", dscores, keys_w, preferred_element_type=jnp.float32)
    grad_kw = jnp.einsum("jhqk,jqhd->jkhd", dscores, q4, preferred_element_type=jnp.float32)
    grad_vw = jnp.einsum("jhqk,jqhd->jkhd", rounded, up4, preferred_element_type=jnp.float32)
    grad_kvw = jnp.concatenate(
        [grad_kw.reshape(unit_count, window, head_cols), grad_vw.reshape(unit_count, window, head_cols)],
        axis=2,
    )
    near_rows = near_keys.shape[0]
    total = jnp.zeros((near_rows, 2 * head_cols), jnp.float32)
    for j in range(unit_count):
        start = rel_starts[j] * UNIT
        total = lax.dynamic_update_slice_in_dim(
            total, lax.dynamic_slice_in_dim(total, start, window, 0) + grad_kvw[j], start, 0
        )
    return grad_q.reshape(rows, head_cols), normed, total


def per_device(heads_in, doc_units):
    section = lax.axis_index("sec")
    seq_place = lax.axis_index("seq")
    is_first = section == 0
    local_heads = heads_in[0]
    _, rows, cols = local_heads.shape
    half = cols // 2
    unit_count = rows // UNIT
    halo_units = MAX_DOC_UNITS - 1
    halo = halo_units * UNIT
    total_cols = cols * lax.axis_size("mp")

    keep_offset = section * half
    send_offset = (1 - section) * half
    sent = lax.dynamic_slice_in_dim(local_heads, send_offset, half, 2)
    kept = lax.dynamic_slice_in_dim(local_heads, keep_offset, half, 2)
    arrived = sec_swap(sent)
    key_value = jnp.where(is_first, kept, arrived)
    query_cot = jnp.where(is_first, arrived, kept)

    joined = jnp.concatenate([key_value[0], key_value[1]], axis=1)
    low, high = halo_swap(joined[:halo], joined[rows - halo :])
    near = jnp.concatenate([low, joined, high], axis=0)

    rel_starts, allowed = window_plan(doc_units, seq_place, unit_count, halo_units)

    def row_total(sums_pair):
        sums = jnp.stack(sums_pair)
        sums = sums + sec_swap(sums)
        sums = sums + lax.ppermute(sums, "mp", [(0, 1), (1, 0)])
        return sums[0], sums[1]

    grad_q, normed, total = attention_grads(
        query_cot[0],
        query_cot[1],
        near[:, :half],
        near[:, half:],
        rel_starts,
        allowed,
        row_total,
        total_cols,
    )
    count = lax.axis_size("seq")
    even = seq_place % 2 == 0
    top = total[:halo].astype(jnp.bfloat16)
    bottom = total[near.shape[0] - halo :].astype(jnp.bfloat16)
    inside = [(i, i ^ 1) for i in range(count) if (i ^ 1) < count]
    between = [(i, i + 1) for i in range(1, count - 1, 2)] + [(i + 1, i) for i in range(1, count - 1, 2)]
    within = lax.ppermute(jnp.where(even, bottom, top), "seq", inside)
    across = lax.ppermute(jnp.where(even, top, bottom), "seq", between)
    middle = total[halo : halo + rows]
    early = rows - halo
    early_even = middle[rows - early :] + within[halo - early :].astype(jnp.float32)
    early_odd = middle[:early] + within[:early].astype(jnp.float32)
    early_own = jnp.where(even, early_even, early_odd).astype(jnp.bfloat16)
    qn_pair = jnp.stack([grad_q.astype(jnp.bfloat16), normed.astype(jnp.bfloat16)])
    early_kv = jnp.stack([early_own[:, :half], early_own[:, half:]])
    early_qn = jnp.where(even, qn_pair[:, rows - early :], qn_pair[:, :early])
    back_early = sec_swap(jnp.where(is_first, early_qn, early_kv))
    back_early, across = lax.optimization_barrier((back_early, across))
    from_left = jnp.where(even, across, within)
    from_right = jnp.where(even, within, across)
    own = (
        middle
        + jnp.pad(from_left.astype(jnp.float32), ((0, rows - halo), (0, 0)))
        + jnp.pad(from_right.astype(jnp.float32), ((rows - halo, 0), (0, 0)))
    )
    late_own = jnp.where(even, own[: rows - early], own[early:]).astype(jnp.bfloat16)
    grad_k = own[:, :half].astype(jnp.bfloat16)
    grad_v = own[:, half:].astype(jnp.bfloat16)
    kv_pair = jnp.stack([grad_k, grad_v])
    late_kv = jnp.stack([late_own[:, :half], late_own[:, half:]])
    late_qn = jnp.where(even, qn_pair[:, : rows - early], qn_pair[:, early:])
    back_late = sec_swap(jnp.where(is_first, late_qn, late_kv))
    back = jnp.where(
        even,
        jnp.concatenate([back_late, back_early], axis=1),
        jnp.concatenate([back_early, back_late], axis=1),
    )
    empty = jnp.zeros_like(kv_pair)
    base = jnp.where(
        is_first,
        jnp.concatenate([kv_pair, empty], axis=2),
        jnp.concatenate([empty, qn_pair], axis=2),
    )
    result = lax.dynamic_update_slice(base, back, (0, 0, jnp.where(is_first, half, 0)))
    return result[None]


def solution(mesh):
    return jax.shard_map(
        per_device,
        mesh=mesh,
        in_specs=(P("sec", None, "seq", "mp"), P()),
        out_specs=P("sec", None, "seq", "mp"),
        check_vma=False,
    )
```

```python
import jax
import jax.numpy as jnp
from jax import lax
from jax.sharding import PartitionSpec as P

UNIT = 128
HEADS = 32
DH = 64
MAX_DOC_UNITS = 3


epsilon = 1e-06


def seq_shift(value, steps):
    count = lax.axis_size("seq")
    initial, last = (max(0, -steps), min(count, count - steps))
    return lax.ppermute(value, "seq", [(source, source + steps) for source in range(initial, last)])


def halo_swap(top, bottom):
    count = lax.axis_size("seq")
    even = lax.axis_index("seq") % 2 == 0
    inside = [(i, i ^ 1) for i in range(count) if (i ^ 1) < count]
    between = [(i, i + 1) for i in range(1, count - 1, 2)] + [(i + 1, i) for i in range(1, count - 1, 2)]
    within = lax.ppermute(jnp.where(even, bottom, top), "seq", inside)
    across = lax.ppermute(jnp.where(even, top, bottom), "seq", between)
    from_below = jnp.where(even, across, within)
    from_above = jnp.where(even, within, across)
    return from_below, from_above


def sec_swap(value):
    return lax.ppermute(value, "sec", [(0, 1), (1, 0)])


def window_plan(doc_units, seq_place, unit_count, halo_units):
    ends = jnp.cumsum(doc_units).astype(jnp.int32)
    first_unit = seq_place * unit_count
    query_units = first_unit + jnp.arange(unit_count, dtype=jnp.int32)

    def unit_doc(units):
        counted = jnp.sum((ends[None, :] <= units[:, None]).astype(jnp.int32), axis=1)
        return jnp.where(units < 0, jnp.int32(-1), counted)

    starts = jnp.max(
        jnp.where(ends[None, :] <= query_units[:, None], ends[None, :], 0), axis=1
    ).astype(jnp.int32)
    key_units = starts[:, None] + jnp.arange(MAX_DOC_UNITS, dtype=jnp.int32)[None, :]
    allowed = unit_doc(key_units.reshape(-1)).reshape(key_units.shape) == unit_doc(query_units)[:, None]
    return starts - (first_unit - halo_units), allowed


def attention_grads(queries, cotangent, near_keys, near_values, rel_starts, allowed, total_fn, total_cols):
    rows, head_cols = queries.shape
    heads = head_cols // DH
    unit_count = rows // UNIT
    window = MAX_DOC_UNITS * UNIT
    score_scale = DH ** (-0.5)

    def windows(near):
        pieces = [
            lax.dynamic_slice_in_dim(near, rel_starts[j] * UNIT, window, 0) for j in range(unit_count)
        ]
        return jnp.stack(pieces).reshape(unit_count, window, heads, DH)

    keys_w = windows(near_keys)
    values_w = windows(near_values)
    q4 = queries.reshape(unit_count, UNIT, heads, DH)
    cot_float = cotangent.astype(jnp.float32)

    mask = jnp.repeat(allowed, UNIT, axis=1)[:, None, None, :]
    scores = (
        jnp.einsum("jqhd,jkhd->jhqk", q4, keys_w, preferred_element_type=jnp.float32) * score_scale
    )
    scores = jnp.where(mask, scores, -jnp.inf)
    row_max = jnp.max(scores, axis=3, keepdims=True)
    expven = jnp.exp(scores - row_max)
    weights = expven / jnp.sum(expven, axis=3, keepdims=True)
    rounded = weights.astype(jnp.bfloat16)
    attended4 = jnp.einsum("jhqk,jkhd->jqhd", rounded, values_w, preferred_element_type=jnp.float32)
    attended = attended4.reshape(rows, head_cols)

    squares, crosses = total_fn(
        (jnp.sum(attended * attended, axis=1), jnp.sum(cot_float * attended, axis=1))
    )
    spread = jnp.sqrt(squares / total_cols + epsilon)
    normed = attended / spread[:, None]
    shared = crosses / total_cols / spread
    upstream = ((cot_float - normed * shared[:, None]) / spread[:, None]).astype(jnp.bfloat16)
    up4 = upstream.reshape(unit_count, UNIT, heads, DH)

    delta = jnp.sum(up4.astype(jnp.float32) * attended4, axis=3)
    delta = jnp.transpose(delta, (0, 2, 1))[..., None]
    dprobs = jnp.einsum("jqhd,jkhd->jhqk", up4, values_w, preferred_element_type=jnp.float32)
    dscores = (weights * (dprobs - delta) * score_scale).astype(jnp.bfloat16)
    grad_q = jnp.einsum("jhqk,jkhd->jqhd", dscores, keys_w, preferred_element_type=jnp.float32)
    grad_kw = jnp.einsum("jhqk,jqhd->jkhd", dscores, q4, preferred_element_type=jnp.float32)
    grad_vw = jnp.einsum("jhqk,jqhd->jkhd", rounded, up4, preferred_element_type=jnp.float32)
    grad_kvw = jnp.concatenate(
        [grad_kw.reshape(unit_count, window, head_cols), grad_vw.reshape(unit_count, window, head_cols)],
        axis=2,
    )
    near_rows = near_keys.shape[0]
    total = jnp.zeros((near_rows, 2 * head_cols), jnp.float32)
    for j in range(unit_count):
        start = rel_starts[j] * UNIT
        total = lax.dynamic_update_slice_in_dim(
            total, lax.dynamic_slice_in_dim(total, start, window, 0) + grad_kvw[j], start, 0
        )
    return grad_q.reshape(rows, head_cols), normed, total


def per_device(heads_in, doc_units):
    section = lax.axis_index("sec")
    seq_place = lax.axis_index("seq")
    is_first = section == 0
    local_heads = heads_in[0]
    _, rows, cols = local_heads.shape
    half = cols // 2
    unit_count = rows // UNIT
    halo_units = MAX_DOC_UNITS - 1
    halo = halo_units * UNIT
    total_cols = cols * lax.axis_size("mp")

    keep_offset = section * half
    send_offset = (1 - section) * half
    sent = lax.dynamic_slice_in_dim(local_heads, send_offset, half, 2)
    kept = lax.dynamic_slice_in_dim(local_heads, keep_offset, half, 2)
    arrived = sec_swap(sent)
    key_value = jnp.where(is_first, kept, arrived)
    query_cot = jnp.where(is_first, arrived, kept)

    joined = jnp.concatenate([key_value[0], key_value[1]], axis=1)
    low, high = halo_swap(joined[:halo], joined[rows - halo :])
    near = jnp.concatenate([low, joined, high], axis=0)

    rel_starts, allowed = window_plan(doc_units, seq_place, unit_count, halo_units)

    def row_total(sums_pair):
        sums = jnp.stack(sums_pair)
        sums = sums + sec_swap(sums)
        sums = sums + lax.ppermute(sums, "mp", [(0, 1), (1, 0)])
        return sums[0], sums[1]

    grad_q, normed, total = attention_grads(
        query_cot[0],
        query_cot[1],
        near[:, :half],
        near[:, half:],
        rel_starts,
        allowed,
        row_total,
        total_cols,
    )
    count = lax.axis_size("seq")
    even = seq_place % 2 == 0
    top = total[:halo].astype(jnp.bfloat16)
    bottom = total[near.shape[0] - halo :].astype(jnp.bfloat16)
    inside = [(i, i ^ 1) for i in range(count) if (i ^ 1) < count]
    between = [(i, i + 1) for i in range(1, count - 1, 2)] + [(i + 1, i) for i in range(1, count - 1, 2)]
    within = lax.ppermute(jnp.where(even, bottom, top), "seq", inside)
    across = lax.ppermute(jnp.where(even, top, bottom), "seq", between)
    middle = total[halo : halo + rows]
    early = rows - halo
    early_even = middle[rows - early :] + within[halo - early :].astype(jnp.float32)
    early_odd = middle[:early] + within[:early].astype(jnp.float32)
    early_own = jnp.where(even, early_even, early_odd).astype(jnp.bfloat16)
    qn_pair = jnp.stack([grad_q.astype(jnp.bfloat16), normed.astype(jnp.bfloat16)])
    early_kv = jnp.stack([early_own[:, :half], early_own[:, half:]])
    early_qn = jnp.where(even, qn_pair[:, rows - early :], qn_pair[:, :early])
    back_early = sec_swap(jnp.where(is_first, early_qn, early_kv))
    back_early, across = lax.optimization_barrier((back_early, across))
    from_left = jnp.where(even, across, within)
    from_right = jnp.where(even, within, across)
    own = (
        middle
        + jnp.pad(from_left.astype(jnp.float32), ((0, rows - halo), (0, 0)))
        + jnp.pad(from_right.astype(jnp.float32), ((rows - halo, 0), (0, 0)))
    )
    late_even = (middle[: rows - early] + across.astype(jnp.float32)) + jnp.pad(
        within[: halo - early].astype(jnp.float32), ((early, 0), (0, 0))
    )
    late_odd = (
        middle[early:] + jnp.pad(within[early:].astype(jnp.float32), ((0, rows - halo), (0, 0)))
    ) + across.astype(jnp.float32)
    late_own = jnp.where(even, late_even, late_odd).astype(jnp.bfloat16)
    grad_k = own[:, :half].astype(jnp.bfloat16)
    grad_v = own[:, half:].astype(jnp.bfloat16)
    kv_pair = jnp.stack([grad_k, grad_v])
    late_kv = jnp.stack([late_own[:, :half], late_own[:, half:]])
    late_qn = jnp.where(even, qn_pair[:, : rows - early], qn_pair[:, early:])
    back_late = sec_swap(jnp.where(is_first, late_qn, late_kv))
    back = jnp.where(
        even,
        jnp.concatenate([back_late, back_early], axis=1),
        jnp.concatenate([back_early, back_late], axis=1),
    )
    result = jnp.where(
        is_first,
        jnp.concatenate([kv_pair, back], axis=2),
        jnp.concatenate([back, qn_pair], axis=2),
    )
    return result[None]


def solution(mesh):
    return jax.shard_map(
        per_device,
        mesh=mesh,
        in_specs=(P("sec", None, "seq", "mp"), P()),
        out_specs=P("sec", None, "seq", "mp"),
        check_vma=False,
    )
```
